128 devices in a mesh: req: 16 (over y, z), head: 8 (over x, core).
Axes of the slice: x: 4, y: 4, z: 4, core: 2. Of those that a mesh axis runs over, the one named last changes fastest.
Arguments:
- hidden_in: bfloat16 [16384, 2048], P('req'), may hold values from -6 to 6
- cache_latent: bfloat16 [16, 512, 512], P('req'), may hold values from -6 to 6
- cache_rope: bfloat16 [16, 512, 64], P('req')
- cache_lengths: int32 [16], P('req'), may hold values from 32 to 512, as said below
- attn_gain: float32 [2048], replicated, may hold values from 0.25 to 1.75
- w_query: bfloat16 [2048, 3072], P(None, 'head'), may hold values from -0.125 to 0.125
- w_latent: bfloat16 [2048, 512], replicated, may hold values from -0.125 to 0.125
- w_latent_rope: bfloat16 [2048, 64], replicated, may hold values from -0.125 to 0.125
- latent_gain: float32 [512], replicated, may hold values from 0.25 to 1.75
- w_key_up: bfloat16 [512, 2048], P(None, 'head'), may hold values from -0.25 to 0.25
- w_value_up: bfloat16 [512, 2048], P(None, 'head'), may hold values from -2 to 2
- w_out: bfloat16 [2048, 2048], P('head'), may hold values from -0.375 to 0.375
- post_gain: float32 [2048], replicated, may hold values from 0.1 to 1.9
- w_router: bfloat16 [2048, 64], replicated
- routes: int32 [16384, 6], P(('req', 'head')), may hold values from 0 to 63, all different within a row; in each aligned block of 128 rows (0 to 127, 128 to 255, ...) at most 14 rows name the same one
- shared_gate: bfloat16 [2048, 2816], P(None, 'head'), may hold values from -0.125 to 0.125
- shared_up: bfloat16 [2048, 2816], P(None, 'head'), may hold values from -0.125 to 0.125
- shared_down: bfloat16 [2816, 2048], P('head')
- expert_gate: bfloat16 [128, 2048, 704], P(('req', 'head')), may hold values from -0.125 to 0.125
- expert_up: bfloat16 [128, 2048, 704], P(('req', 'head')), may hold values from -0.125 to 0.125
- expert_down: bfloat16 [128, 704, 2048], P(('req', 'head')), may hold values from -0.875 to 0.875
Outputs:
- layer_out: bfloat16 [16384, 2048], P(('req', 'head'))
The draws below stay inside these ranges and needn't reach their ends.
Inputs may be any that keep to these rules, and one draw needn't show every extreme that they name: `cache_lengths`: two requests have exactly 512 cached rows; each other request has between 32 and 64. `routes`: the 6 experts of a row differ; within each aligned block of 128 rows (the rows of one device) no expert is named more than 14 times.
All inputs are finite; a program needn't handle non-finite values.
Results may differ from the reference program's by a relative error of at most 0.025.
The reference program's roundings to bfloat16 on the way count: a program that leaves them out, or rounds other values in their place, can miss the bound.
Values may be sent and summed in bfloat16 or wider, within the bound.
No kernel may reach another device: no remote copies, remote signals or barrier semaphores. Data moves between devices by JAX's collectives and lax.ppermute only.
A program may use at most 192 MiB of HBM per device.

```python
import math
import jax
import jax.numpy as jnp
import numpy as np
from jax import lax

D = 2048
HEADS = 16
NOPE = 128
ROPE = 64
VDIM = 128
LATENT = 512
EXPERTS = 64
TOPK = 6
FF = 1408
TOK_DEV = 128
CACHE_MAX = 512
SHARED_FF = 2816
HEAD_DEV = 2
REQS = 16
STRETCH = 1024
TOKENS = 16384
CAP = 14
EXP_SPLIT = 2
EXP_ROWS = 128
FF_PART = 704


def draw_cache_lengths(key, part):
    key_short, key_pick = jax.random.split(key)
    shorter = jax.random.randint(key_short, (REQS,), CACHE_MAX // 16, CACHE_MAX // 8 + 1, dtype=jnp.int32)
    picked = jax.random.permutation(key_pick, REQS)[:2]
    longest = jnp.zeros((REQS,), jnp.int32).at[picked].set(1)
    return jnp.where(longest == 1, CACHE_MAX, shorter).astype(jnp.int32)


def draw_cache_rope(key, part):
    key_base = jax.random.fold_in(key, 0)
    return jnp.clip(jax.random.normal(key_base, (REQS, CACHE_MAX, ROPE), jnp.float32), -5.0, 5.0).astype(jnp.bfloat16)


def draw_w_router(key, part):
    key_base = jax.random.fold_in(key, 0)
    return (jnp.clip(jax.random.normal(key_base, (D, EXPERTS), jnp.float32), -5.0, 5.0) * D ** (-0.5)).astype(jnp.bfloat16)


def draw_shared_down(key, part):
    fraction = jnp.arange(SHARED_FF, dtype=jnp.float32) / (SHARED_FF - 1)
    base_values = jnp.clip(jax.random.normal(key, (SHARED_FF, D), jnp.float32), -5.0, 5.0)
    rising = jnp.exp(fraction * math.log(4.0))
    return (base_values * rising[:, None] * SHARED_FF ** (-0.5)).astype(jnp.bfloat16)


def steps_of(own_key, extent, cuts, low, largest):
    factor_of = 1.0
    for position, shards_of in cuts:
        draws = jax.random.uniform(jax.random.fold_in(jax.random.fold_in(own_key, 6), position), (shards_of,), jnp.float32, low / len(cuts), largest / len(cuts))
        factor_of = factor_of * jnp.repeat(jnp.exp(draws), extent[position] // shards_of).reshape((-1,) + (1,) * (len(extent) - 1 - position))
    return factor_of


def assign_block(rng, own, number, rows, count, top, most, slope):
    ranking = jax.random.permutation(rng, count)
    heavy_load, common = shares(count, rows * top, most, slope, True), shares(count, rows * top, most, slope, False)
    places = jnp.arange(count)

    def named(sizes, rotation):
        used = int((sizes > 0).sum())
        fixed = max(1, used // 4)
        shifted = fixed + (places - fixed + rotation * (used - fixed)) % max(1, count - fixed)
        return jnp.zeros((count,), jnp.int32).at[ranking[jnp.where(places < fixed, places, shifted)]].set(jnp.asarray(sizes, jnp.int32))

    sizes = jnp.where(number % 4 == 0, named(heavy_load, number // 4), named(common, number - number // 4 - 1))
    mixed = jax.random.permutation(jax.random.fold_in(own, 3), count)
    donor, taker = mixed[0:count // 2 * 2:2], mixed[1:count // 2 * 2:2]
    slack = jnp.minimum(sizes[donor] - 1, most - sizes[taker]) // 2
    slack = jnp.where((donor == ranking[0]) | (taker == ranking[0]) | (sizes[taker] == 0), 0, jnp.maximum(slack, 0))
    shifted = jax.random.randint(jax.random.fold_in(own, 4), (count // 2,), 0, 1 << 20) % (slack + 1)
    sizes = sizes.at[donor].add(-shifted).at[taker].add(shifted)
    members = jnp.searchsorted(jnp.cumsum(sizes), jnp.arange(rows * top), side="right").astype(jnp.int32)
    grid = members.reshape(top, rows).T
    grid = grid[jax.random.permutation(jax.random.fold_in(own, 1), rows)]
    rotation = jax.random.randint(jax.random.fold_in(own, 2), (rows, 1), 0, top)
    return jnp.take_along_axis(grid, (jnp.arange(top)[None, :] + rotation) % top, axis=1)


def shares(amount, total, most, skew, full):
    loads = [(1 << 20) // math.isqrt(rank ** skew) + 1 for rank in range(1, amount + 1)]
    largest = most if full else min(most, max(-(-total // amount), total * loads[0] // sum(loads)))
    least = 1 if total - largest >= amount - 1 else 0
    counts, rest = [largest] + [least] * (amount - 1), total - largest - least * (amount - 1)
    while rest > 0:
        movable = [i for i in range(1, amount) if counts[i] < largest] or [i for i in range(1, amount) if counts[i] < most]
        whole, left = sum([loads[i] for i in movable]), rest
        for i in movable:
            addition = min(most - counts[i], max(1, left * loads[i] // whole), rest)
            counts[i] = counts[i] + addition
            rest = rest - addition
    return np.array(counts)


def centred(own_key, shape, scale, most, cuts=(), kind=jnp.bfloat16):
    values = jax.random.normal(own_key, shape, jnp.float32) * scale
    if len(cuts) > 0:
        values = steps_of(own_key, shape, cuts, -0.22, 0.18) * values
    return jnp.clip(values, min=-most, max=most).astype(kind)


def setup_inputs(seed: int = 0) -> dict:
    keys = jax.random.split(jax.random.key(seed), 22)
    hidden_in = centred(keys[0], (TOKENS, D), 1.0, 6.0, ((0, 16),))
    cache_latent = centred(keys[1], (REQS, CACHE_MAX, LATENT), 1.0, 6.0, ((0, 16),))
    cache_rope = draw_cache_rope(jax.random.fold_in(keys[21], 71), 0)
    cache_lengths = draw_cache_lengths(jax.random.fold_in(keys[21], 71), 0)
    attn_gain = jnp.clip(1.0 + 0.15 * jax.random.normal(keys[4], (D,), jnp.float32), 0.25, 1.75)
    w_query = centred(keys[5], (D, HEADS * (NOPE + ROPE)), D ** -0.5, 0.125, ((1, 8),))
    w_latent = centred(keys[6], (D, LATENT), D ** -0.5, 0.125)
    w_latent_rope = centred(keys[7], (D, ROPE), D ** -0.5, 0.125)
    latent_gain = jnp.clip(1.0 + 0.15 * jax.random.normal(keys[8], (LATENT,), jnp.float32), 0.25, 1.75)
    w_key_up = centred(keys[9], (LATENT, HEADS * NOPE), LATENT ** -0.5, 0.25, ((1, 8),))
    w_value_up = centred(keys[10], (LATENT, HEADS * VDIM), (max(1, LATENT // 64)) ** -0.5, 2.0, ((1, 8),))
    w_out = centred(keys[11], (HEADS * VDIM, D), (HEADS * VDIM // 8) ** -0.5, 0.375, ((0, 8),))
    post_gain = jnp.clip(1.0 + 0.18 * jax.random.normal(keys[12], (D,), jnp.float32), 0.1, 1.9)
    w_router = draw_w_router(jax.random.fold_in(keys[21], 71), 0)
    routes_keys = jax.random.split(jax.random.fold_in(keys[14], 1), TOKENS // TOK_DEV)
    routes_turns = jax.random.permutation(jax.random.fold_in(keys[14], 3), TOKENS // TOK_DEV)
    routes = jax.vmap(lambda own, number: assign_block(jax.random.fold_in(keys[14], 2), own, number, TOK_DEV, EXPERTS, TOPK, CAP, 2))(routes_keys, routes_turns).reshape((TOKENS, TOPK))
    shared_gate = centred(keys[15], (D, SHARED_FF), D ** -0.5, 0.125, ((1, 8),))
    shared_up = centred(keys[16], (D, SHARED_FF), D ** -0.5, 0.125, ((1, 8),))
    shared_down = draw_shared_down(jax.random.fold_in(keys[21], 71), 0)
    expert_gate = centred(keys[18], (EXP_ROWS, D, FF_PART), D ** -0.5, 0.125, ((0, 128),))
    expert_up = centred(keys[19], (EXP_ROWS, D, FF_PART), D ** -0.5, 0.125, ((0, 128),))
    expert_down = centred(keys[20], (EXP_ROWS, FF_PART, D), (max(1, FF // 32)) ** -0.5, 0.875, ((0, 128),))
    return {"hidden_in": hidden_in, "cache_latent": cache_latent, "cache_rope": cache_rope, "cache_lengths": cache_lengths, "attn_gain": attn_gain, "w_query": w_query, "w_latent": w_latent, "w_latent_rope": w_latent_rope, "latent_gain": latent_gain, "w_key_up": w_key_up, "w_value_up": w_value_up, "w_out": w_out, "post_gain": post_gain, "w_router": w_router, "routes": routes, "shared_gate": shared_gate, "shared_up": shared_up, "shared_down": shared_down, "expert_gate": expert_gate, "expert_up": expert_up, "expert_down": expert_down}


def rms_scale(values, gain_row):
    return values * lax.rsqrt(lax.optimization_barrier(jnp.mean(values * values, axis=-1, keepdims=True)) + 1e-06) * gain_row

def rotate(values, positions):
    half_size = values.shape[-1] // 2
    frequency = jnp.exp(jnp.arange(half_size, dtype=jnp.float32) * (-2.0 * math.log(10000.0) / values.shape[-1]))
    angles = positions.astype(jnp.float32)[:, None] * frequency[None, :]
    shape_mid = (angles.shape[0],) + (1,) * (values.ndim - 2) + (half_size,)
    cosine = jnp.cos(angles).reshape(shape_mid)
    sine_part = jnp.sin(angles).reshape(shape_mid)
    first_half = values[..., :half_size]
    second_half = values[..., half_size:]
    return jnp.concatenate([first_half * cosine - second_half * sine_part, second_half * cosine + first_half * sine_part], axis=-1)

def round_trip(values):
    return lax.optimization_barrier(values.astype(jnp.bfloat16)).astype(jnp.float32)

def reference(hidden_in, cache_latent, cache_rope, cache_lengths, attn_gain, w_query, w_latent, w_latent_rope, latent_gain, w_key_up, w_value_up, w_out, post_gain, w_router, routes, shared_gate, shared_up, shared_down, expert_gate, expert_up, expert_down):
    score_scale = (NOPE + ROPE) ** (-0.5)
    key_up = w_key_up.reshape(LATENT, HEADS, NOPE).astype(jnp.float32)
    value_up = w_value_up.reshape(LATENT, HEADS, VDIM).astype(jnp.float32)
    out_groups = w_out.reshape(HEADS // HEAD_DEV, HEAD_DEV * VDIM, D).astype(jnp.float32)
    key_index = jnp.arange(CACHE_MAX + STRETCH, dtype=jnp.int32)
    query_index = jnp.arange(STRETCH, dtype=jnp.int32)

    def request_layer(inputs):
        tokens_in, lat_cache, rope_cache, length = inputs
        normed_in = rms_scale(tokens_in.astype(jnp.float32), attn_gain).astype(jnp.bfloat16)
        positions = length + query_index
        query_all = jnp.dot(normed_in, w_query, preferred_element_type=jnp.float32).reshape(STRETCH, HEADS, NOPE + ROPE)
        query_nope = query_all[..., :NOPE].astype(jnp.bfloat16)
        query_rope = rotate(query_all[..., NOPE:], positions).astype(jnp.bfloat16)
        new_latent = rms_scale(jnp.dot(normed_in, w_latent, preferred_element_type=jnp.float32), latent_gain).astype(jnp.bfloat16)
        new_rope = rotate(jnp.dot(normed_in, w_latent_rope, preferred_element_type=jnp.float32), positions).astype(jnp.bfloat16)
        absorbed = jnp.einsum('chn,lhn->chl', query_nope.astype(jnp.float32), key_up).astype(jnp.bfloat16)
        keys_latent = jnp.concatenate([lat_cache, new_latent], axis=0).astype(jnp.float32)
        keys_rope = jnp.concatenate([rope_cache, new_rope], axis=0).astype(jnp.float32)
        scores = (jnp.einsum('chl,kl->chk', absorbed.astype(jnp.float32), keys_latent) + jnp.einsum('chr,kr->chk', query_rope.astype(jnp.float32), keys_rope)) * score_scale
        visible = jnp.where(key_index[None, :] < CACHE_MAX, key_index[None, :] < length, key_index[None, :] - CACHE_MAX <= query_index[:, None])[:, None, :]
        masked = jnp.where(visible, scores, -jnp.inf)
        row_max = lax.optimization_barrier(jnp.max(masked, axis=-1, keepdims=True))
        exponent = jnp.where(visible, jnp.exp(masked - row_max), 0.0)
        row_total = lax.optimization_barrier(jnp.sum(exponent, axis=-1, keepdims=True))
        latent_out = (jnp.einsum('chk,kl->chl', round_trip(exponent), keys_latent) / row_total).astype(jnp.bfloat16)
        head_out = jnp.einsum('chl,lhv->chv', latent_out.astype(jnp.float32), value_up).astype(jnp.bfloat16)
        group_terms = jnp.einsum('cgk,gkd->gcd', head_out.reshape(STRETCH, HEADS // HEAD_DEV, HEAD_DEV * VDIM).astype(jnp.float32), out_groups)
        attn_sum = lax.optimization_barrier(jnp.sum(round_trip(group_terms), axis=0))
        residual = (tokens_in.astype(jnp.float32) + attn_sum).astype(jnp.bfloat16)
        normed = rms_scale(residual.astype(jnp.float32), post_gain).astype(jnp.bfloat16)
        shared_act = (jax.nn.silu(jnp.dot(normed, shared_gate, preferred_element_type=jnp.float32)) * jnp.dot(normed, shared_up, preferred_element_type=jnp.float32)).astype(jnp.bfloat16)
        shared_out = jnp.dot(shared_act, shared_down, preferred_element_type=jnp.float32)
        return (residual, normed, shared_out)
    residual_all, normed_all, shared_all = lax.map(request_layer, (hidden_in.reshape(REQS, STRETCH, D), cache_latent, cache_rope, cache_lengths))
    residual_all = residual_all.reshape(TOKENS, D)
    normed_all = normed_all.reshape(TOKENS, D)
    shared_all = shared_all.reshape(TOKENS, D)
    logits = jnp.dot(normed_all, w_router, preferred_element_type=jnp.float32)
    chosen = jnp.take_along_axis(logits, routes, axis=1)
    route_weight = jax.nn.softmax(chosen, axis=-1)
    sources = TOKENS // TOK_DEV
    expert_ids = routes.reshape(sources, TOK_DEV * TOPK)
    onehot = (expert_ids[:, :, None] == jnp.arange(EXPERTS, dtype=jnp.int32)[None, None, :]).astype(jnp.int32)
    slot_of = lax.optimization_barrier(jnp.sum((jnp.cumsum(onehot, axis=1) - onehot) * onehot, axis=-1))
    table_index = ((expert_ids * sources + jnp.arange(sources, dtype=jnp.int32)[:, None]) * CAP + slot_of).reshape(-1).astype(jnp.int32)
    token_of = jnp.full((EXPERTS * sources * CAP,), TOKENS, jnp.int32).at[table_index].set(jnp.arange(TOKENS * TOPK, dtype=jnp.int32) // TOPK)
    weight_of = jnp.zeros((EXPERTS * sources * CAP,), jnp.float32).at[table_index].set(route_weight.reshape(-1))
    normed_pad = jnp.concatenate([normed_all, jnp.zeros((1, D), jnp.bfloat16)], axis=0)

    def expert_step(running, expert):
        first_slot = (expert * (sources * CAP)).astype(jnp.int32)
        slot_tokens = lax.dynamic_slice_in_dim(token_of, first_slot, sources * CAP)
        slot_weights = lax.dynamic_slice_in_dim(weight_of, first_slot, sources * CAP)
        inputs = normed_pad[slot_tokens]
        first_row = (expert * EXP_SPLIT).astype(jnp.int32)
        gate_full = lax.dynamic_slice_in_dim(expert_gate, first_row, EXP_SPLIT, 0).transpose(1, 0, 2).reshape(D, FF)
        up_full = lax.dynamic_slice_in_dim(expert_up, first_row, EXP_SPLIT, 0).transpose(1, 0, 2).reshape(D, FF)
        down_full = lax.dynamic_slice_in_dim(expert_down, first_row, EXP_SPLIT, 0).reshape(FF, D)
        activation = (jax.nn.silu(jnp.dot(inputs, gate_full, preferred_element_type=jnp.float32)) * jnp.dot(inputs, up_full, preferred_element_type=jnp.float32)).astype(jnp.bfloat16)
        expert_rows = jnp.dot(activation, down_full, preferred_element_type=jnp.float32)
        running = running.at[slot_tokens].add(slot_weights[:, None] * round_trip(expert_rows))
        return (running, None)
    routed = lax.scan(expert_step, jnp.zeros((TOKENS + 1, D), jnp.float32), jnp.arange(EXPERTS, dtype=jnp.int32))[0][:TOKENS]
    return (residual_all.astype(jnp.float32) + shared_all + routed).astype(jnp.bfloat16)
```

```python
import math

import jax
import jax.numpy as jnp
from jax import lax
from jax.sharding import PartitionSpec as P

NOPE = 128
ROPE = 64
VDIM = 128
LATENT = 512
EXPERTS = 64
CAP = 14


def rms_scale(values, gain_row):
    return values * lax.rsqrt(jnp.mean(values * values, axis=-1, keepdims=True) + 1e-06) * gain_row


def rotate(values, positions):
    half_size = values.shape[-1] // 2
    frequency = jnp.exp(
        jnp.arange(half_size, dtype=jnp.float32) * (-2.0 * math.log(10000.0) / values.shape[-1])
    )
    angles = positions.astype(jnp.float32)[:, None] * frequency[None, :]
    shape_mid = (angles.shape[0],) + (1,) * (values.ndim - 2) + (half_size,)
    cosine = jnp.cos(angles).reshape(shape_mid)
    sine_part = jnp.sin(angles).reshape(shape_mid)
    first_half = values[..., :half_size]
    second_half = values[..., half_size:]
    return jnp.concatenate(
        [
            first_half * cosine - second_half * sine_part,
            second_half * cosine + first_half * sine_part,
        ],
        axis=-1,
    )


def attend_rows(
    absorbed, query_rope, first_row, cache_lat, cache_keys, length, new_latent, new_rope, block_rows
):
    query_count = absorbed.shape[0]
    head_count = absorbed.shape[1]
    latent_width = absorbed.shape[2]
    score_scale = (NOPE + ROPE) ** (-0.5)

    def update(state_now, keys_latent, keys_rope, visible):
        row_max, row_total, weighted = state_now
        scores = (
            jnp.einsum("qhl,kl->qhk", absorbed, keys_latent, preferred_element_type=jnp.float32)
            + jnp.einsum("qhr,kr->qhk", query_rope, keys_rope, preferred_element_type=jnp.float32)
        ) * score_scale
        scores = jnp.where(visible, scores, -jnp.inf)
        new_max = jnp.maximum(row_max, jnp.max(scores, axis=-1))
        exponent = jnp.exp(scores - new_max[..., None])
        factor = jnp.exp(row_max - new_max)
        row_total = row_total * factor + jnp.sum(exponent, axis=-1)
        weighted = weighted * factor[..., None] + jnp.einsum(
            "qhk,kl->qhl",
            exponent.astype(jnp.bfloat16),
            keys_latent,
            preferred_element_type=jnp.float32,
        )
        return (new_max, row_total, weighted)

    initial = (
        jnp.full((query_count, head_count), -jnp.inf, jnp.float32),
        jnp.zeros((query_count, head_count), jnp.float32),
        jnp.zeros((query_count, head_count, latent_width), jnp.float32),
    )
    cache_block = min(128, cache_lat.shape[0])
    block_total = (length + cache_block - 1) // cache_block

    def cache_step(block_index, state_now):
        start_row = block_index * cache_block
        keys_latent = lax.dynamic_slice_in_dim(cache_lat, start_row, cache_block, 0)
        keys_rope = lax.dynamic_slice_in_dim(cache_keys, start_row, cache_block, 0)
        visible = (start_row + jnp.arange(cache_block, dtype=jnp.int32) < length)[None, None, :]
        return update(state_now, keys_latent, keys_rope, visible)

    state_now = lax.fori_loop(0, block_total, cache_step, initial)
    query_pos = first_row + jnp.arange(query_count, dtype=jnp.int32)
    for key_block in range(first_row // block_rows + 1):
        key_start = key_block * block_rows
        visible = (key_start + jnp.arange(block_rows, dtype=jnp.int32))[None, None, :] <= query_pos[
            :, None, None
        ]
        state_now = update(
            state_now,
            new_latent[key_start : key_start + block_rows],
            new_rope[key_start : key_start + block_rows],
            visible,
        )
    row_max, row_total, weighted = state_now
    return (weighted / row_total[..., None]).astype(jnp.bfloat16)


def per_device(
    hidden_in,
    cache_latent,
    cache_rope,
    cache_lengths,
    attn_gain,
    w_query,
    w_latent,
    w_latent_rope,
    latent_gain,
    w_key_up,
    w_value_up,
    w_out,
    post_gain,
    w_router,
    routes,
    shared_gate,
    shared_up,
    shared_down,
    expert_gate,
    expert_up,
    expert_down,
):
    request_rows = hidden_in.shape[0]
    model_width = hidden_in.shape[1]
    row_count = routes.shape[0]
    top_count = routes.shape[1]
    head_local = w_query.shape[1] // (NOPE + ROPE)
    length = cache_lengths[0]
    chip_count = lax.axis_size("hx")
    core_count = lax.axis_size("hc")
    chip_index = lax.axis_index("hx")
    core_index = lax.axis_index("hc")
    normed_in = rms_scale(hidden_in.astype(jnp.float32), attn_gain).astype(jnp.bfloat16)
    positions = length + jnp.arange(request_rows, dtype=jnp.int32)
    query_all = jnp.dot(normed_in, w_query, preferred_element_type=jnp.float32).reshape(
        request_rows, head_local, NOPE + ROPE
    )
    query_nope = query_all[..., :NOPE].astype(jnp.bfloat16)
    query_rope = rotate(query_all[..., NOPE:], positions).astype(jnp.bfloat16)
    new_latent = rms_scale(
        jnp.dot(normed_in, w_latent, preferred_element_type=jnp.float32), latent_gain
    ).astype(jnp.bfloat16)
    new_rope = rotate(
        jnp.dot(normed_in, w_latent_rope, preferred_element_type=jnp.float32), positions
    ).astype(jnp.bfloat16)
    key_up = w_key_up.reshape(LATENT, head_local, NOPE)
    absorbed = jnp.einsum(
        "chn,lhn->chl", query_nope, key_up, preferred_element_type=jnp.float32
    ).astype(jnp.bfloat16)
    value_up = w_value_up.reshape(LATENT, head_local, VDIM)
    block_rows = min(512, request_rows)
    outputs = []
    for first_row in range(0, request_rows, block_rows):
        latent_out = attend_rows(
            absorbed[first_row : first_row + block_rows],
            query_rope[first_row : first_row + block_rows],
            first_row,
            cache_latent[0],
            cache_rope[0],
            length,
            new_latent,
            new_rope,
            block_rows,
        )
        head_out = jnp.einsum(
            "qhl,lhv->qhv", latent_out, value_up, preferred_element_type=jnp.float32
        ).astype(jnp.bfloat16)
        outputs.append(head_out.reshape(block_rows, head_local * VDIM))
    head_rows = jnp.concatenate(outputs, axis=0)
    def core_major(values):
        return (
            values.reshape(chip_count, core_count, row_count, -1)
            .transpose(1, 0, 2, 3)
            .reshape(request_rows, -1)
        )

    head_perm = core_major(head_rows)
    attn_term = jnp.dot(head_perm, w_out, preferred_element_type=jnp.float32).astype(jnp.bfloat16)
    attn_half = lax.psum_scatter(
        attn_term.astype(jnp.float32), "hc", scatter_dimension=0, tiled=True
    ).astype(jnp.bfloat16)
    attn_half = lax.psum(attn_half, "hx")
    attn_sum = lax.all_gather(attn_half, "hc", axis=0, tiled=True).astype(jnp.float32)
    residual = (core_major(hidden_in).astype(jnp.float32) + attn_sum).astype(jnp.bfloat16)
    normed = rms_scale(residual.astype(jnp.float32), post_gain).astype(jnp.bfloat16)
    shared_act = (
        jax.nn.silu(jnp.dot(normed, shared_gate, preferred_element_type=jnp.float32))
        * jnp.dot(normed, shared_up, preferred_element_type=jnp.float32)
    ).astype(jnp.bfloat16)
    shared_part = jnp.dot(shared_act, shared_down, preferred_element_type=jnp.float32)
    shared_core = lax.psum_scatter(shared_part, "hc", scatter_dimension=0, tiled=True)
    shared_own = lax.psum_scatter(
        shared_core.astype(jnp.bfloat16), "hx", scatter_dimension=0, tiled=True
    ).astype(jnp.float32)
    own_start = (core_index * chip_count + chip_index) * row_count
    residual_own = lax.dynamic_slice_in_dim(residual, own_start, row_count, 0)
    normed_own = lax.dynamic_slice_in_dim(normed, own_start, row_count, 0)
    experts = EXPERTS
    capacity = CAP
    slot_total = experts * capacity
    logits = jnp.dot(normed_own, w_router, preferred_element_type=jnp.float32)
    matches = routes[:, :, None] == jnp.arange(experts, dtype=jnp.int32)[None, None, :]
    chosen = jnp.sum(jnp.where(matches, logits[:, None, :], 0.0), axis=-1)
    route_weight = jax.nn.softmax(chosen, axis=-1)
    pair_hits = matches.reshape(row_count * top_count, experts).astype(jnp.int32)
    pair_ranks = jnp.cumsum(pair_hits, axis=0) - pair_hits
    slot_of = jnp.sum(pair_ranks * pair_hits, axis=-1)
    target = (routes.reshape(-1) * capacity + slot_of).reshape(row_count, top_count)
    slot_ids = jnp.arange(slot_total, dtype=jnp.int32)
    hit = target[:, :, None] == slot_ids[None, None, :]
    dispatch = jnp.any(hit, axis=1).astype(jnp.bfloat16)
    send_rows = jnp.einsum(
        "ts,td->sd", dispatch, normed_own, preferred_element_type=jnp.float32
    ).astype(jnp.bfloat16)
    devices = lax.axis_size(("req", "hx", "hc"))
    piece = slot_total // devices
    outgoing = send_rows.reshape(devices, piece, model_width)
    arrived = lax.all_to_all(
        outgoing, ("req", "hx", "hc"), split_axis=0, concat_axis=0, tiled=True
    ).reshape(devices * piece, model_width)
    swap = [(0, 1), (1, 0)]
    partner = lax.ppermute(arrived, "hc", swap)

    def expert_part(rows):
        gate_values = jnp.dot(rows, expert_gate[0], preferred_element_type=jnp.float32)
        upward = jnp.dot(rows, expert_up[0], preferred_element_type=jnp.float32)
        activation = (jax.nn.silu(gate_values) * upward).astype(jnp.bfloat16)
        return jnp.dot(activation, expert_down[0], preferred_element_type=jnp.float32)

    own_part = expert_part(arrived)
    partner_part = expert_part(partner)
    partner_back = lax.ppermute(partner_part.astype(jnp.bfloat16), "hc", swap)
    expert_done = (own_part + partner_back.astype(jnp.float32)).astype(jnp.bfloat16)
    returned = lax.all_to_all(
        expert_done.reshape(devices, piece, model_width),
        ("req", "hx", "hc"),
        split_axis=0,
        concat_axis=0,
        tiled=True,
    ).reshape(slot_total, model_width)
    combine = jnp.sum(jnp.where(hit, route_weight[:, :, None], 0.0), axis=1)
    routed = jnp.dot(
        combine,
        returned.astype(jnp.float32),
        precision=lax.Precision.HIGHEST,
        preferred_element_type=jnp.float32,
    )
    return (residual_own.astype(jnp.float32) + shared_own + routed).astype(jnp.bfloat16)


def solution(mesh):
    core_count = 2
    split_mesh = jax.sharding.Mesh(
        mesh.devices.reshape(
            mesh.shape["req"], mesh.shape["head"] // core_count, core_count
        ),
        ("req", "hx", "hc"),
    )
    head = ("hx", "hc")
    every = ("req", "hx", "hc")
    in_specs = (
        P("req", None),
        P("req", None, None),
        P("req", None, None),
        P("req"),
        P(),
        P(None, head),
        P(),
        P(),
        P(),
        P(None, head),
        P(None, head),
        P(head, None),
        P(),
        P(),
        P(every, None),
        P(None, head),
        P(None, head),
        P(head, None),
        P(every, None, None),
        P(every, None, None),
        P(every, None, None),
    )
    out_specs = P(every, None)
    return jax.shard_map(
        per_device, mesh=split_mesh, in_specs=in_specs, out_specs=out_specs, check_vma=False
    )
```

```python
import math

import jax
import jax.numpy as jnp
from jax import lax
from jax.sharding import PartitionSpec as P

NOPE = 128
ROPE = 64
VDIM = 128
LATENT = 512
EXPERTS = 64
CAP = 14


def rms_scale(values, gain_row):
    return values * lax.rsqrt(jnp.mean(values * values, axis=-1, keepdims=True) + 1e-06) * gain_row


def rotate(values, positions):
    half_size = values.shape[-1] // 2
    frequency = jnp.exp(
        jnp.arange(half_size, dtype=jnp.float32) * (-2.0 * math.log(10000.0) / values.shape[-1])
    )
    angles = positions.astype(jnp.float32)[:, None] * frequency[None, :]
    shape_mid = (angles.shape[0],) + (1,) * (values.ndim - 2) + (half_size,)
    cosine = jnp.cos(angles).reshape(shape_mid)
    sine_part = jnp.sin(angles).reshape(shape_mid)
    first_half = values[..., :half_size]
    second_half = values[..., half_size:]
    return jnp.concatenate(
        [
            first_half * cosine - second_half * sine_part,
            second_half * cosine + first_half * sine_part,
        ],
        axis=-1,
    )


def attend_rows(
    absorbed, query_rope, first_row, cache_lat, cache_keys, length, new_latent, new_rope, block_rows
):
    query_count = absorbed.shape[0]
    head_count = absorbed.shape[1]
    latent_width = absorbed.shape[2]
    score_scale = (NOPE + ROPE) ** (-0.5)

    def update(state_now, keys_latent, keys_rope, visible):
        row_max, row_total, weighted = state_now
        scores = (
            jnp.einsum("qhl,kl->qhk", absorbed, keys_latent, preferred_element_type=jnp.float32)
            + jnp.einsum("qhr,kr->qhk", query_rope, keys_rope, preferred_element_type=jnp.float32)
        ) * score_scale
        scores = jnp.where(visible, scores, -jnp.inf)
        new_max = jnp.maximum(row_max, jnp.max(scores, axis=-1))
        exponent = jnp.exp(scores - new_max[..., None])
        factor = jnp.exp(row_max - new_max)
        row_total = row_total * factor + jnp.sum(exponent, axis=-1)
        weighted = weighted * factor[..., None] + jnp.einsum(
            "qhk,kl->qhl",
            exponent.astype(jnp.bfloat16),
            keys_latent,
            preferred_element_type=jnp.float32,
        )
        return (new_max, row_total, weighted)

    initial = (
        jnp.full((query_count, head_count), -jnp.inf, jnp.float32),
        jnp.zeros((query_count, head_count), jnp.float32),
        jnp.zeros((query_count, head_count, latent_width), jnp.float32),
    )
    cache_block = min(128, cache_lat.shape[0])
    block_total = (length + cache_block - 1) // cache_block

    def cache_step(block_index, state_now):
        start_row = block_index * cache_block
        keys_latent = lax.dynamic_slice_in_dim(cache_lat, start_row, cache_block, 0)
        keys_rope = lax.dynamic_slice_in_dim(cache_keys, start_row, cache_block, 0)
        visible = (start_row + jnp.arange(cache_block, dtype=jnp.int32) < length)[None, None, :]
        return update(state_now, keys_latent, keys_rope, visible)

    state_now = lax.fori_loop(0, block_total, cache_step, initial)
    query_pos = first_row + jnp.arange(query_count, dtype=jnp.int32)
    for key_block in range(first_row // block_rows + 1):
        key_start = key_block * block_rows
        visible = (key_start + jnp.arange(block_rows, dtype=jnp.int32))[None, None, :] <= query_pos[
            :, None, None
        ]
        state_now = update(
            state_now,
            new_latent[key_start : key_start + block_rows],
            new_rope[key_start : key_start + block_rows],
            visible,
        )
    row_max, row_total, weighted = state_now
    return (weighted / row_total[..., None]).astype(jnp.bfloat16)


def per_device(
    hidden_in,
    cache_latent,
    cache_rope,
    cache_lengths,
    attn_gain,
    w_query,
    w_latent,
    w_latent_rope,
    latent_gain,
    w_key_up,
    w_value_up,
    w_out,
    post_gain,
    w_router,
    routes,
    shared_gate,
    shared_up,
    shared_down,
    expert_gate,
    expert_up,
    expert_down,
):
    request_rows = hidden_in.shape[0]
    model_width = hidden_in.shape[1]
    row_count = routes.shape[0]
    top_count = routes.shape[1]
    head_local = w_query.shape[1] // (NOPE + ROPE)
    length = cache_lengths[0]
    chip_count = lax.axis_size("hx")
    core_count = lax.axis_size("hc")
    chip_index = lax.axis_index("hx")
    core_index = lax.axis_index("hc")
    normed_in = rms_scale(hidden_in.astype(jnp.float32), attn_gain).astype(jnp.bfloat16)
    positions = length + jnp.arange(request_rows, dtype=jnp.int32)
    query_all = jnp.dot(normed_in, w_query, preferred_element_type=jnp.float32).reshape(
        request_rows, head_local, NOPE + ROPE
    )
    query_nope = query_all[..., :NOPE].astype(jnp.bfloat16)
    query_rope = rotate(query_all[..., NOPE:], positions).astype(jnp.bfloat16)
    new_latent = rms_scale(
        jnp.dot(normed_in, w_latent, preferred_element_type=jnp.float32), latent_gain
    ).astype(jnp.bfloat16)
    new_rope = rotate(
        jnp.dot(normed_in, w_latent_rope, preferred_element_type=jnp.float32), positions
    ).astype(jnp.bfloat16)
    key_up = w_key_up.reshape(LATENT, head_local, NOPE)
    absorbed = jnp.einsum(
        "chn,lhn->chl", query_nope, key_up, preferred_element_type=jnp.float32
    ).astype(jnp.bfloat16)
    value_up = w_value_up.reshape(LATENT, head_local, VDIM)
    block_rows = min(512, request_rows)
    outputs = []
    for first_row in range(0, request_rows, block_rows):
        latent_out = attend_rows(
            absorbed[first_row : first_row + block_rows],
            query_rope[first_row : first_row + block_rows],
            first_row,
            cache_latent[0],
            cache_rope[0],
            length,
            new_latent,
            new_rope,
            block_rows,
        )
        head_out = jnp.einsum(
            "qhl,lhv->qhv", latent_out, value_up, preferred_element_type=jnp.float32
        ).astype(jnp.bfloat16)
        outputs.append(head_out.reshape(block_rows, head_local * VDIM))
    head_rows = jnp.concatenate(outputs, axis=0)
    head_count = chip_count * core_count
    head_index = chip_index * core_count + core_index
    attn_term = jnp.dot(head_rows, w_out, preferred_element_type=jnp.float32).astype(jnp.bfloat16)
    attn_parts = lax.all_to_all(
        attn_term.reshape(head_count, row_count, model_width),
        ("hx", "hc"),
        split_axis=0,
        concat_axis=0,
        tiled=True,
    )
    attn_own = jnp.sum(attn_parts.astype(jnp.float32), axis=0)
    own_start = head_index * row_count
    hidden_own = lax.dynamic_slice_in_dim(hidden_in, own_start, row_count, 0)
    residual_own = (hidden_own.astype(jnp.float32) + attn_own).astype(jnp.bfloat16)
    normed_own = rms_scale(residual_own.astype(jnp.float32), post_gain).astype(jnp.bfloat16)
    normed_chips = lax.all_gather(normed_own, "hx", axis=0, tiled=True)
    normed = lax.all_gather(normed_chips, "hc", axis=0, tiled=True)
    shared_act = (
        jax.nn.silu(jnp.dot(normed, shared_gate, preferred_element_type=jnp.float32))
        * jnp.dot(normed, shared_up, preferred_element_type=jnp.float32)
    ).astype(jnp.bfloat16)
    shared_part = jnp.dot(shared_act, shared_down, preferred_element_type=jnp.float32)
    shared_core = lax.psum_scatter(shared_part, "hc", scatter_dimension=0, tiled=True)
    shared_own = lax.psum_scatter(
        shared_core.astype(jnp.bfloat16), "hx", scatter_dimension=0, tiled=True
    ).astype(jnp.float32)
    experts = EXPERTS
    capacity = CAP
    logits = jnp.dot(normed_own, w_router, preferred_element_type=jnp.float32)
    matches = routes[:, :, None] == jnp.arange(experts, dtype=jnp.int32)[None, None, :]
    chosen = jnp.sum(jnp.where(matches, logits[:, None, :], 0.0), axis=-1)
    route_weight = jax.nn.softmax(chosen, axis=-1)
    pair_hits = matches.reshape(row_count * top_count, experts).astype(jnp.int32)
    pair_ranks = jnp.cumsum(pair_hits, axis=0) - pair_hits
    slot_of = jnp.sum(pair_ranks * pair_hits, axis=-1)
    target = (routes.reshape(-1) * capacity + slot_of).reshape(row_count, top_count)
    devices = lax.axis_size(("req", "hx", "hc"))
    piece = experts * capacity // devices
    dest_ids = jnp.arange(devices, dtype=jnp.int32)[:, None] * piece + jnp.arange(
        piece, dtype=jnp.int32
    )[None, :]
    hit = target[:, :, None, None] == dest_ids[None, None, :, :]
    dispatch = jnp.any(hit, axis=1).astype(jnp.bfloat16)
    outgoing = jnp.einsum(
        "tpj,td->pjd", dispatch, normed_own, preferred_element_type=jnp.float32
    ).astype(jnp.bfloat16)
    arrived = lax.all_to_all(
        outgoing, ("req", "hx", "hc"), split_axis=0, concat_axis=0, tiled=True
    )
    swap = [(0, 1), (1, 0)]
    partner = lax.ppermute(arrived, "hc", swap)

    def expert_part(rows):
        gate_values = jnp.einsum(
            "pjd,df->pjf", rows, expert_gate[0], preferred_element_type=jnp.float32
        )
        upward = jnp.einsum("pjd,df->pjf", rows, expert_up[0], preferred_element_type=jnp.float32)
        activation = (jax.nn.silu(gate_values) * upward).astype(jnp.bfloat16)
        return jnp.einsum(
            "pjf,fd->pjd", activation, expert_down[0], preferred_element_type=jnp.float32
        )

    own_part = expert_part(arrived)
    partner_part = expert_part(partner)
    partner_back = lax.ppermute(partner_part.astype(jnp.bfloat16), "hc", swap)
    expert_done = (own_part + partner_back.astype(jnp.float32)).astype(jnp.bfloat16)
    returned = lax.all_to_all(
        expert_done, ("req", "hx", "hc"), split_axis=0, concat_axis=0, tiled=True
    )
    combine = jnp.sum(jnp.where(hit, route_weight[:, :, None, None], 0.0), axis=1)
    routed = jnp.einsum(
        "tpj,pjd->td",
        combine,
        returned.astype(jnp.float32),
        precision=lax.Precision.HIGHEST,
        preferred_element_type=jnp.float32,
    )
    return (residual_own.astype(jnp.float32) + shared_own + routed).astype(jnp.bfloat16)


def solution(mesh):
    core_count = 2
    split_mesh = jax.sharding.Mesh(
        mesh.devices.reshape(
            mesh.shape["req"], mesh.shape["head"] // core_count, core_count
        ),
        ("req", "hx", "hc"),
    )
    head = ("hx", "hc")
    every = ("req", "hx", "hc")
    in_specs = (
        P("req", None),
        P("req", None, None),
        P("req", None, None),
        P("req"),
        P(),
        P(None, head),
        P(),
        P(),
        P(),
        P(None, head),
        P(None, head),
        P(head, None),
        P(),
        P(),
        P(every, None),
        P(None, head),
        P(None, head),
        P(head, None),
        P(every, None, None),
        P(every, None, None),
        P(every, None, None),
    )
    out_specs = P(every, None)
    return jax.shard_map(
        per_device, mesh=split_mesh, in_specs=in_specs, out_specs=out_specs, check_vma=False
    )
```

```python
import math

import jax
import jax.numpy as jnp
from jax import lax
from jax.sharding import PartitionSpec as P

NOPE = 128
ROPE = 64
VDIM = 128
LATENT = 512
EXPERTS = 64
CAP = 14


def rms_scale(values, gain_row):
    return values * lax.rsqrt(jnp.mean(values * values, axis=-1, keepdims=True) + 1e-06) * gain_row


def rotate(values, positions):
    half_size = values.shape[-1] // 2
    frequency = jnp.exp(
        jnp.arange(half_size, dtype=jnp.float32) * (-2.0 * math.log(10000.0) / values.shape[-1])
    )
    angles = positions.astype(jnp.float32)[:, None] * frequency[None, :]
    shape_mid = (angles.shape[0],) + (1,) * (values.ndim - 2) + (half_size,)
    cosine = jnp.cos(angles).reshape(shape_mid)
    sine_part = jnp.sin(angles).reshape(shape_mid)
    first_half = values[..., :half_size]
    second_half = values[..., half_size:]
    return jnp.concatenate(
        [
            first_half * cosine - second_half * sine_part,
            second_half * cosine + first_half * sine_part,
        ],
        axis=-1,
    )


def attend_rows(
    absorbed, query_rope, first_row, cache_lat, cache_keys, length, new_latent, new_rope, block_rows
):
    query_count = absorbed.shape[0]
    head_count = absorbed.shape[1]
    latent_width = absorbed.shape[2]
    score_scale = (NOPE + ROPE) ** (-0.5)

    def update(state_now, keys_latent, keys_rope, visible):
        row_max, row_total, weighted = state_now
        scores = (
            jnp.einsum("qhl,kl->qhk", absorbed, keys_latent, preferred_element_type=jnp.float32)
            + jnp.einsum("qhr,kr->qhk", query_rope, keys_rope, preferred_element_type=jnp.float32)
        ) * score_scale
        scores = jnp.where(visible, scores, -jnp.inf)
        new_max = jnp.maximum(row_max, jnp.max(scores, axis=-1))
        exponent = jnp.exp(scores - new_max[..., None])
        factor = jnp.exp(row_max - new_max)
        row_total = row_total * factor + jnp.sum(exponent, axis=-1)
        weighted = weighted * factor[..., None] + jnp.einsum(
            "qhk,kl->qhl",
            exponent.astype(jnp.bfloat16),
            keys_latent,
            preferred_element_type=jnp.float32,
        )
        return (new_max, row_total, weighted)

    initial = (
        jnp.full((query_count, head_count), -jnp.inf, jnp.float32),
        jnp.zeros((query_count, head_count), jnp.float32),
        jnp.zeros((query_count, head_count, latent_width), jnp.float32),
    )
    cache_block = min(128, cache_lat.shape[0])
    block_total = (length + cache_block - 1) // cache_block

    def cache_step(block_index, state_now):
        start_row = block_index * cache_block
        keys_latent = lax.dynamic_slice_in_dim(cache_lat, start_row, cache_block, 0)
        keys_rope = lax.dynamic_slice_in_dim(cache_keys, start_row, cache_block, 0)
        visible = (start_row + jnp.arange(cache_block, dtype=jnp.int32) < length)[None, None, :]
        return update(state_now, keys_latent, keys_rope, visible)

    state_now = lax.fori_loop(0, block_total, cache_step, initial)
    query_pos = first_row + jnp.arange(query_count, dtype=jnp.int32)
    for key_block in range(first_row // block_rows + 1):
        key_start = key_block * block_rows
        visible = (key_start + jnp.arange(block_rows, dtype=jnp.int32))[None, None, :] <= query_pos[
            :, None, None
        ]
        state_now = update(
            state_now,
            new_latent[key_start : key_start + block_rows],
            new_rope[key_start : key_start + block_rows],
            visible,
        )
    row_max, row_total, weighted = state_now
    return (weighted / row_total[..., None]).astype(jnp.bfloat16)


def per_device(
    hidden_in,
    cache_latent,
    cache_rope,
    cache_lengths,
    attn_gain,
    w_query,
    w_latent,
    w_latent_rope,
    latent_gain,
    w_key_up,
    w_value_up,
    w_out,
    post_gain,
    w_router,
    routes,
    shared_gate,
    shared_up,
    shared_down,
    expert_gate,
    expert_up,
    expert_down,
):
    request_rows = hidden_in.shape[0]
    model_width = hidden_in.shape[1]
    row_count = routes.shape[0]
    top_count = routes.shape[1]
    head_local = w_query.shape[1] // (NOPE + ROPE)
    length = cache_lengths[0]
    chip_count = lax.axis_size("hx")
    core_count = lax.axis_size("hc")
    chip_index = lax.axis_index("hx")
    core_index = lax.axis_index("hc")
    normed_in = rms_scale(hidden_in.astype(jnp.float32), attn_gain).astype(jnp.bfloat16)
    positions = length + jnp.arange(request_rows, dtype=jnp.int32)
    query_all = jnp.dot(normed_in, w_query, preferred_element_type=jnp.float32).reshape(
        request_rows, head_local, NOPE + ROPE
    )
    query_nope = query_all[..., :NOPE].astype(jnp.bfloat16)
    query_rope = rotate(query_all[..., NOPE:], positions).astype(jnp.bfloat16)
    new_latent = rms_scale(
        jnp.dot(normed_in, w_latent, preferred_element_type=jnp.float32), latent_gain
    ).astype(jnp.bfloat16)
    new_rope = rotate(
        jnp.dot(normed_in, w_latent_rope, preferred_element_type=jnp.float32), positions
    ).astype(jnp.bfloat16)
    key_up = w_key_up.reshape(LATENT, head_local, NOPE)
    absorbed = jnp.einsum(
        "chn,lhn->chl", query_nope, key_up, preferred_element_type=jnp.float32
    ).astype(jnp.bfloat16)
    value_up = w_value_up.reshape(LATENT, head_local, VDIM)
    block_rows = min(512, request_rows)
    outputs = []
    for first_row in range(0, request_rows, block_rows):
        latent_out = attend_rows(
            absorbed[first_row : first_row + block_rows],
            query_rope[first_row : first_row + block_rows],
            first_row,
            cache_latent[0],
            cache_rope[0],
            length,
            new_latent,
            new_rope,
            block_rows,
        )
        head_out = jnp.einsum(
            "qhl,lhv->qhv", latent_out, value_up, preferred_element_type=jnp.float32
        ).astype(jnp.bfloat16)
        outputs.append(head_out.reshape(block_rows, head_local * VDIM))
    head_rows = jnp.concatenate(outputs, axis=0)
    head_count = chip_count * core_count
    head_index = chip_index * core_count + core_index
    attn_term = jnp.dot(head_rows, w_out, preferred_element_type=jnp.float32).astype(jnp.bfloat16)
    attn_parts = lax.all_to_all(
        attn_term.reshape(head_count, row_count, model_width),
        ("hx", "hc"),
        split_axis=0,
        concat_axis=0,
        tiled=True,
    )
    attn_own = jnp.sum(attn_parts.astype(jnp.float32), axis=0)
    own_start = head_index * row_count
    hidden_own = lax.dynamic_slice_in_dim(hidden_in, own_start, row_count, 0)
    residual_own = (hidden_own.astype(jnp.float32) + attn_own).astype(jnp.bfloat16)
    normed_own = rms_scale(residual_own.astype(jnp.float32), post_gain).astype(jnp.bfloat16)
    normed_all = lax.all_gather(normed_own, ("hx", "hc"), axis=0, tiled=True)
    experts = EXPERTS
    capacity = CAP
    logits = jnp.dot(normed_own, w_router, preferred_element_type=jnp.float32)
    matches = routes[:, :, None] == jnp.arange(experts, dtype=jnp.int32)[None, None, :]
    chosen = jnp.sum(jnp.where(matches, logits[:, None, :], 0.0), axis=-1)
    route_weight = jax.nn.softmax(chosen, axis=-1)
    pair_hits = matches.reshape(row_count * top_count, experts).astype(jnp.int32)
    pair_ranks = jnp.cumsum(pair_hits, axis=0) - pair_hits
    slot_of = jnp.sum(pair_ranks * pair_hits, axis=-1)
    target = (routes.reshape(-1) * capacity + slot_of).reshape(row_count, top_count)
    devices = lax.axis_size(("req", "hx", "hc"))
    piece = experts * capacity // devices
    dest_ids = jnp.arange(devices, dtype=jnp.int32)[:, None] * piece + jnp.arange(
        piece, dtype=jnp.int32
    )[None, :]
    hit = target[:, :, None, None] == dest_ids[None, None, :, :]
    dispatch = jnp.any(hit, axis=1).astype(jnp.bfloat16)
    outgoing = jnp.einsum(
        "tpj,td->pjd", dispatch, normed_own, preferred_element_type=jnp.float32
    ).astype(jnp.bfloat16)
    arrived = lax.all_to_all(
        outgoing, ("req", "hx", "hc"), split_axis=0, concat_axis=0, tiled=True
    )
    normed_all, arrived = lax.optimization_barrier((normed_all, arrived))
    normed = (
        normed_all.reshape(chip_count, core_count, row_count, model_width)
        .transpose(1, 0, 2, 3)
        .reshape(request_rows, model_width)
    )
    shared_act = (
        jax.nn.silu(jnp.dot(normed, shared_gate, preferred_element_type=jnp.float32))
        * jnp.dot(normed, shared_up, preferred_element_type=jnp.float32)
    ).astype(jnp.bfloat16)
    shared_part = jnp.dot(shared_act, shared_down, preferred_element_type=jnp.float32)
    shared_core = lax.psum_scatter(shared_part, "hc", scatter_dimension=0, tiled=True)
    shared_own = lax.psum_scatter(
        shared_core.astype(jnp.bfloat16), "hx", scatter_dimension=0, tiled=True
    ).astype(jnp.float32)
    swap = [(0, 1), (1, 0)]
    partner = lax.ppermute(arrived, "hc", swap)

    def expert_part(rows):
        gate_values = jnp.einsum(
            "pjd,df->pjf", rows, expert_gate[0], preferred_element_type=jnp.float32
        )
        upward = jnp.einsum("pjd,df->pjf", rows, expert_up[0], preferred_element_type=jnp.float32)
        activation = (jax.nn.silu(gate_values) * upward).astype(jnp.bfloat16)
        return jnp.einsum(
            "pjf,fd->pjd", activation, expert_down[0], preferred_element_type=jnp.float32
        )

    own_part = expert_part(arrived)
    partner_part = expert_part(partner)
    partner_back = lax.ppermute(partner_part.astype(jnp.bfloat16), "hc", swap)
    expert_done = (own_part + partner_back.astype(jnp.float32)).astype(jnp.bfloat16)
    returned = lax.all_to_all(
        expert_done, ("req", "hx", "hc"), split_axis=0, concat_axis=0, tiled=True
    )
    combine = jnp.sum(jnp.where(hit, route_weight[:, :, None, None], 0.0), axis=1)
    routed = jnp.einsum(
        "tpj,pjd->td",
        combine,
        returned.astype(jnp.float32),
        precision=lax.Precision.HIGHEST,
        preferred_element_type=jnp.float32,
    )
    return (residual_own.astype(jnp.float32) + shared_own + routed).astype(jnp.bfloat16)


def solution(mesh):
    core_count = 2
    split_mesh = jax.sharding.Mesh(
        mesh.devices.reshape(
            mesh.shape["req"], mesh.shape["head"] // core_count, core_count
        ),
        ("req", "hx", "hc"),
    )
    head = ("hx", "hc")
    every = ("req", "hx", "hc")
    in_specs = (
        P("req", None),
        P("req", None, None),
        P("req", None, None),
        P("req"),
        P(),
        P(None, head),
        P(),
        P(),
        P(),
        P(None, head),
        P(None, head),
        P(head, None),
        P(),
        P(),
        P(every, None),
        P(None, head),
        P(None, head),
        P(head, None),
        P(every, None, None),
        P(every, None, None),
        P(every, None, None),
    )
    out_specs = P(every, None)
    return jax.shard_map(
        per_device, mesh=split_mesh, in_specs=in_specs, out_specs=out_specs, check_vma=False
    )
```

```python
import math

import jax
import jax.numpy as jnp
from jax import lax
from jax.sharding import PartitionSpec as P

NOPE = 128
ROPE = 64
VDIM = 128
LATENT = 512
EXPERTS = 64
CAP = 14


def rms_scale(values, gain_row):
    return values * lax.rsqrt(jnp.mean(values * values, axis=-1, keepdims=True) + 1e-06) * gain_row


def rotate(values, positions):
    half_size = values.shape[-1] // 2
    frequency = jnp.exp(
        jnp.arange(half_size, dtype=jnp.float32) * (-2.0 * math.log(10000.0) / values.shape[-1])
    )
    angles = positions.astype(jnp.float32)[:, None] * frequency[None, :]
    shape_mid = (angles.shape[0],) + (1,) * (values.ndim - 2) + (half_size,)
    cosine = jnp.cos(angles).reshape(shape_mid)
    sine_part = jnp.sin(angles).reshape(shape_mid)
    first_half = values[..., :half_size]
    second_half = values[..., half_size:]
    return jnp.concatenate(
        [
            first_half * cosine - second_half * sine_part,
            second_half * cosine + first_half * sine_part,
        ],
        axis=-1,
    )


def attend_rows(absorbed, query_rope, first_row, cache_lat, cache_keys, length, new_latent, new_rope):
    query_count = absorbed.shape[0]
    cache_rows = cache_lat.shape[0]
    score_scale = (NOPE + ROPE) ** (-0.5)
    seen_new = first_row + query_count
    keys_latent = jnp.concatenate([cache_lat, new_latent[:seen_new]], axis=0)
    keys_rope = jnp.concatenate([cache_keys, new_rope[:seen_new]], axis=0)
    scores = (
        jnp.einsum("qhl,kl->qhk", absorbed, keys_latent, preferred_element_type=jnp.float32)
        + jnp.einsum("qhr,kr->qhk", query_rope, keys_rope, preferred_element_type=jnp.float32)
    ) * score_scale
    key_index = jnp.arange(cache_rows + seen_new, dtype=jnp.int32)[None, :]
    query_pos = first_row + jnp.arange(query_count, dtype=jnp.int32)[:, None]
    visible = jnp.where(
        key_index < cache_rows, key_index < length, key_index - cache_rows <= query_pos
    )
    scores = jnp.where(visible[:, None, :], scores, -jnp.inf)
    row_max = jnp.max(scores, axis=-1)
    exponent = jnp.exp(scores - row_max[..., None])
    row_total = jnp.sum(exponent, axis=-1)
    weighted = jnp.einsum(
        "qhk,kl->qhl",
        exponent.astype(jnp.bfloat16),
        keys_latent,
        preferred_element_type=jnp.float32,
    )
    return (weighted / row_total[..., None]).astype(jnp.bfloat16)


def per_device(
    hidden_in,
    cache_latent,
    cache_rope,
    cache_lengths,
    attn_gain,
    w_query,
    w_latent,
    w_latent_rope,
    latent_gain,
    w_key_up,
    w_value_up,
    w_out,
    post_gain,
    w_router,
    routes,
    shared_gate,
    shared_up,
    shared_down,
    expert_gate,
    expert_up,
    expert_down,
):
    request_rows = hidden_in.shape[0]
    model_width = hidden_in.shape[1]
    row_count = routes.shape[0]
    top_count = routes.shape[1]
    head_local = w_query.shape[1] // (NOPE + ROPE)
    length = cache_lengths[0]
    chip_count = lax.axis_size("hx")
    core_count = lax.axis_size("hc")
    chip_index = lax.axis_index("hx")
    core_index = lax.axis_index("hc")
    normed_in = rms_scale(hidden_in.astype(jnp.float32), attn_gain).astype(jnp.bfloat16)
    positions = length + jnp.arange(request_rows, dtype=jnp.int32)
    query_all = jnp.dot(normed_in, w_query, preferred_element_type=jnp.float32).reshape(
        request_rows, head_local, NOPE + ROPE
    )
    query_nope = query_all[..., :NOPE].astype(jnp.bfloat16)
    query_rope = rotate(query_all[..., NOPE:], positions).astype(jnp.bfloat16)
    new_latent = rms_scale(
        jnp.dot(normed_in, w_latent, preferred_element_type=jnp.float32), latent_gain
    ).astype(jnp.bfloat16)
    new_rope = rotate(
        jnp.dot(normed_in, w_latent_rope, preferred_element_type=jnp.float32), positions
    ).astype(jnp.bfloat16)
    key_up = w_key_up.reshape(LATENT, head_local, NOPE)
    absorbed = jnp.einsum(
        "chn,lhn->chl", query_nope, key_up, preferred_element_type=jnp.float32
    ).astype(jnp.bfloat16)
    value_up = w_value_up.reshape(LATENT, head_local, VDIM)
    block_rows = min(512, request_rows)
    outputs = []
    for first_row in range(0, request_rows, block_rows):
        latent_out = attend_rows(
            absorbed[first_row : first_row + block_rows],
            query_rope[first_row : first_row + block_rows],
            first_row,
            cache_latent[0],
            cache_rope[0],
            length,
            new_latent,
            new_rope,
        )
        head_out = jnp.einsum(
            "qhl,lhv->qhv", latent_out, value_up, preferred_element_type=jnp.float32
        ).astype(jnp.bfloat16)
        outputs.append(head_out.reshape(block_rows, head_local * VDIM))
    head_rows = jnp.concatenate(outputs, axis=0)
    head_count = chip_count * core_count
    head_index = chip_index * core_count + core_index
    attn_term = jnp.dot(head_rows, w_out, preferred_element_type=jnp.float32).astype(jnp.bfloat16)
    attn_parts = lax.all_to_all(
        attn_term.reshape(head_count, row_count, model_width),
        ("hx", "hc"),
        split_axis=0,
        concat_axis=0,
        tiled=True,
    )
    attn_own = jnp.sum(attn_parts.astype(jnp.float32), axis=0)
    own_start = head_index * row_count
    hidden_own = lax.dynamic_slice_in_dim(hidden_in, own_start, row_count, 0)
    residual_own = (hidden_own.astype(jnp.float32) + attn_own).astype(jnp.bfloat16)
    normed_own = rms_scale(residual_own.astype(jnp.float32), post_gain).astype(jnp.bfloat16)
    normed_all = lax.all_gather(normed_own, ("hx", "hc"), axis=0, tiled=True)
    experts = EXPERTS
    capacity = CAP
    logits = jnp.dot(normed_own, w_router, preferred_element_type=jnp.float32)
    matches = routes[:, :, None] == jnp.arange(experts, dtype=jnp.int32)[None, None, :]
    chosen = jnp.sum(jnp.where(matches, logits[:, None, :], 0.0), axis=-1)
    route_weight = jax.nn.softmax(chosen, axis=-1)
    pair_hits = matches.reshape(row_count * top_count, experts).astype(jnp.int32)
    pair_ranks = jnp.cumsum(pair_hits, axis=0) - pair_hits
    slot_of = jnp.sum(pair_ranks * pair_hits, axis=-1)
    target = (routes.reshape(-1) * capacity + slot_of).reshape(row_count, top_count)
    devices = lax.axis_size(("req", "hx", "hc"))
    piece = experts * capacity // devices
    dest_ids = jnp.arange(devices, dtype=jnp.int32)[:, None] * piece + jnp.arange(
        piece, dtype=jnp.int32
    )[None, :]
    hit = target[:, :, None, None] == dest_ids[None, None, :, :]
    dispatch = jnp.any(hit, axis=1).astype(jnp.bfloat16)
    outgoing = jnp.einsum(
        "tpj,td->pjd", dispatch, normed_own, preferred_element_type=jnp.float32
    ).astype(jnp.bfloat16)
    arrived = lax.all_to_all(
        outgoing, ("req", "hx", "hc"), split_axis=0, concat_axis=0, tiled=True
    )
    normed_all, arrived = lax.optimization_barrier((normed_all, arrived))
    normed = (
        normed_all.reshape(chip_count, core_count, row_count, model_width)
        .transpose(1, 0, 2, 3)
        .reshape(request_rows, model_width)
    )
    shared_act = (
        jax.nn.silu(jnp.dot(normed, shared_gate, preferred_element_type=jnp.float32))
        * jnp.dot(normed, shared_up, preferred_element_type=jnp.float32)
    ).astype(jnp.bfloat16)
    shared_part = jnp.dot(shared_act, shared_down, preferred_element_type=jnp.float32)
    shared_core = lax.psum_scatter(shared_part, "hc", scatter_dimension=0, tiled=True)
    shared_own = lax.psum_scatter(
        shared_core.astype(jnp.bfloat16), "hx", scatter_dimension=0, tiled=True
    ).astype(jnp.float32)
    swap = [(0, 1), (1, 0)]
    partner = lax.ppermute(arrived, "hc", swap)

    def expert_part(rows):
        gate_values = jnp.einsum(
            "pjd,df->pjf", rows, expert_gate[0], preferred_element_type=jnp.float32
        )
        upward = jnp.einsum("pjd,df->pjf", rows, expert_up[0], preferred_element_type=jnp.float32)
        activation = (jax.nn.silu(gate_values) * upward).astype(jnp.bfloat16)
        return jnp.einsum(
            "pjf,fd->pjd", activation, expert_down[0], preferred_element_type=jnp.float32
        )

    own_part = expert_part(arrived)
    partner_part = expert_part(partner)
    partner_back = lax.ppermute(partner_part.astype(jnp.bfloat16), "hc", swap)
    expert_done = (own_part + partner_back.astype(jnp.float32)).astype(jnp.bfloat16)
    returned = lax.all_to_all(
        expert_done, ("req", "hx", "hc"), split_axis=0, concat_axis=0, tiled=True
    )
    combine = jnp.sum(jnp.where(hit, route_weight[:, :, None, None], 0.0), axis=1)
    routed = jnp.einsum(
        "tpj,pjd->td",
        combine,
        returned.astype(jnp.float32),
        precision=lax.Precision.HIGHEST,
        preferred_element_type=jnp.float32,
    )
    return (residual_own.astype(jnp.float32) + shared_own + routed).astype(jnp.bfloat16)


def solution(mesh):
    core_count = 2
    split_mesh = jax.sharding.Mesh(
        mesh.devices.reshape(
            mesh.shape["req"], mesh.shape["head"] // core_count, core_count
        ),
        ("req", "hx", "hc"),
    )
    head = ("hx", "hc")
    every = ("req", "hx", "hc")
    in_specs = (
        P("req", None),
        P("req", None, None),
        P("req", None, None),
        P("req"),
        P(),
        P(None, head),
        P(),
        P(),
        P(),
        P(None, head),
        P(None, head),
        P(head, None),
        P(),
        P(),
        P(every, None),
        P(None, head),
        P(None, head),
        P(head, None),
        P(every, None, None),
        P(every, None, None),
        P(every, None, None),
    )
    out_specs = P(every, None)
    return jax.shard_map(
        per_device, mesh=split_mesh, in_specs=in_specs, out_specs=out_specs, check_vma=False
    )
```

```python
import math

import jax
import jax.numpy as jnp
from jax import lax
from jax.sharding import PartitionSpec as P

NOPE = 128
ROPE = 64
VDIM = 128
LATENT = 512
EXPERTS = 64
CAP = 14


def rms_scale(values, gain_row):
    return values * lax.rsqrt(jnp.mean(values * values, axis=-1, keepdims=True) + 1e-06) * gain_row


def rotate(values, positions):
    half_size = values.shape[-1] // 2
    frequency = jnp.exp(
        jnp.arange(half_size, dtype=jnp.float32) * (-2.0 * math.log(10000.0) / values.shape[-1])
    )
    angles = positions.astype(jnp.float32)[:, None] * frequency[None, :]
    shape_mid = (angles.shape[0],) + (1,) * (values.ndim - 2) + (half_size,)
    cosine = jnp.cos(angles).reshape(shape_mid)
    sine_part = jnp.sin(angles).reshape(shape_mid)
    first_half = values[..., :half_size]
    second_half = values[..., half_size:]
    return jnp.concatenate(
        [
            first_half * cosine - second_half * sine_part,
            second_half * cosine + first_half * sine_part,
        ],
        axis=-1,
    )


def attend_rows(absorbed, query_rope, first_row, cache_lat, cache_keys, length, new_latent, new_rope):
    query_count = absorbed.shape[0]
    cache_rows = cache_lat.shape[0]
    score_scale = (NOPE + ROPE) ** (-0.5)
    seen_new = first_row + query_count
    keys_latent = jnp.concatenate([cache_lat, new_latent[:seen_new]], axis=0)
    keys_rope = jnp.concatenate([cache_keys, new_rope[:seen_new]], axis=0)
    scores = (
        jnp.einsum("qhl,kl->qhk", absorbed, keys_latent, preferred_element_type=jnp.float32)
        + jnp.einsum("qhr,kr->qhk", query_rope, keys_rope, preferred_element_type=jnp.float32)
    ) * score_scale
    key_index = jnp.arange(cache_rows + seen_new, dtype=jnp.int32)[None, :]
    query_pos = first_row + jnp.arange(query_count, dtype=jnp.int32)[:, None]
    visible = jnp.where(
        key_index < cache_rows, key_index < length, key_index - cache_rows <= query_pos
    )
    scores = jnp.where(visible[:, None, :], scores, -jnp.inf)
    row_max = jnp.max(scores, axis=-1)
    exponent = jnp.exp(scores - row_max[..., None])
    row_total = jnp.sum(exponent, axis=-1)
    weighted = jnp.einsum(
        "qhk,kl->qhl",
        exponent.astype(jnp.bfloat16),
        keys_latent,
        preferred_element_type=jnp.float32,
    )
    return (weighted / row_total[..., None]).astype(jnp.bfloat16)


def per_device(
    hidden_in,
    cache_latent,
    cache_rope,
    cache_lengths,
    attn_gain,
    w_query,
    w_latent,
    w_latent_rope,
    latent_gain,
    w_key_up,
    w_value_up,
    w_out,
    post_gain,
    w_router,
    routes,
    shared_gate,
    shared_up,
    shared_down,
    expert_gate,
    expert_up,
    expert_down,
):
    request_rows = hidden_in.shape[0]
    model_width = hidden_in.shape[1]
    row_count = routes.shape[0]
    top_count = routes.shape[1]
    head_local = w_query.shape[1] // (NOPE + ROPE)
    length = cache_lengths[0]
    chip_count = lax.axis_size("hx")
    core_count = lax.axis_size("hc")
    chip_index = lax.axis_index("hx")
    core_index = lax.axis_index("hc")
    normed_in = rms_scale(hidden_in.astype(jnp.float32), attn_gain).astype(jnp.bfloat16)
    positions = length + jnp.arange(request_rows, dtype=jnp.int32)
    query_all = jnp.dot(normed_in, w_query, preferred_element_type=jnp.float32).reshape(
        request_rows, head_local, NOPE + ROPE
    )
    query_nope = query_all[..., :NOPE].astype(jnp.bfloat16)
    query_rope = rotate(query_all[..., NOPE:], positions).astype(jnp.bfloat16)
    new_latent = rms_scale(
        jnp.dot(normed_in, w_latent, preferred_element_type=jnp.float32), latent_gain
    ).astype(jnp.bfloat16)
    new_rope = rotate(
        jnp.dot(normed_in, w_latent_rope, preferred_element_type=jnp.float32), positions
    ).astype(jnp.bfloat16)
    key_up = w_key_up.reshape(LATENT, head_local, NOPE)
    absorbed = jnp.einsum(
        "chn,lhn->chl", query_nope, key_up, preferred_element_type=jnp.float32
    ).astype(jnp.bfloat16)
    value_up = w_value_up.reshape(LATENT, head_local, VDIM)
    block_rows = min(512, request_rows)
    outputs = []
    for first_row in range(0, request_rows, block_rows):
        latent_out = attend_rows(
            absorbed[first_row : first_row + block_rows],
            query_rope[first_row : first_row + block_rows],
            first_row,
            cache_latent[0],
            cache_rope[0],
            length,
            new_latent,
            new_rope,
        )
        head_out = jnp.einsum(
            "qhl,lhv->qhv", latent_out, value_up, preferred_element_type=jnp.float32
        ).astype(jnp.bfloat16)
        outputs.append(head_out.reshape(block_rows, head_local * VDIM))
    head_rows = jnp.concatenate(outputs, axis=0)
    head_count = chip_count * core_count
    head_index = chip_index * core_count + core_index
    attn_term = jnp.dot(head_rows, w_out, preferred_element_type=jnp.float32).astype(jnp.bfloat16)
    attn_parts = lax.all_to_all(
        attn_term.reshape(head_count, row_count, model_width),
        ("hx", "hc"),
        split_axis=0,
        concat_axis=0,
        tiled=True,
    )
    attn_own = jnp.sum(attn_parts.astype(jnp.float32), axis=0)
    own_start = head_index * row_count
    hidden_own = lax.dynamic_slice_in_dim(hidden_in, own_start, row_count, 0)
    residual_own = (hidden_own.astype(jnp.float32) + attn_own).astype(jnp.bfloat16)
    normed_own = rms_scale(residual_own.astype(jnp.float32), post_gain).astype(jnp.bfloat16)
    normed_all = lax.all_gather(normed_own, ("hx", "hc"), axis=0, tiled=True)
    experts = EXPERTS
    capacity = CAP
    logits = jnp.dot(normed_own, w_router, preferred_element_type=jnp.float32)
    matches = routes[:, :, None] == jnp.arange(experts, dtype=jnp.int32)[None, None, :]
    chosen = jnp.sum(jnp.where(matches, logits[:, None, :], 0.0), axis=-1)
    route_weight = jax.nn.softmax(chosen, axis=-1)
    pair_hits = matches.reshape(row_count * top_count, experts).astype(jnp.int32)
    pair_ranks = jnp.cumsum(pair_hits, axis=0) - pair_hits
    slot_of = jnp.sum(pair_ranks * pair_hits, axis=-1)
    slot_width = -(-capacity // 16) * 16
    target = (routes.reshape(-1) * slot_width + slot_of).reshape(row_count, top_count)
    chips = ("req", "hx")
    chip_total = lax.axis_size(chips)
    dest_ids = jnp.arange(chip_total, dtype=jnp.int32)[:, None] * slot_width + jnp.arange(
        slot_width, dtype=jnp.int32
    )[None, :]
    hit = target[:, :, None, None] == dest_ids[None, None, :, :]
    dispatch = jnp.any(hit, axis=1).astype(jnp.bfloat16)
    outgoing = jnp.einsum(
        "tpj,td->pjd", dispatch, normed_own, preferred_element_type=jnp.float32
    ).astype(jnp.bfloat16)
    arrived = lax.all_to_all(outgoing, chips, split_axis=0, concat_axis=0, tiled=True)
    normed_all, arrived = lax.optimization_barrier((normed_all, arrived))
    normed = (
        normed_all.reshape(chip_count, core_count, row_count, model_width)
        .transpose(1, 0, 2, 3)
        .reshape(request_rows, model_width)
    )
    shared_act = (
        jax.nn.silu(jnp.dot(normed, shared_gate, preferred_element_type=jnp.float32))
        * jnp.dot(normed, shared_up, preferred_element_type=jnp.float32)
    ).astype(jnp.bfloat16)
    shared_part = jnp.dot(shared_act, shared_down, preferred_element_type=jnp.float32)
    shared_core = lax.psum_scatter(shared_part, "hc", scatter_dimension=0, tiled=True)
    shared_own = lax.psum_scatter(
        shared_core.astype(jnp.bfloat16), "hx", scatter_dimension=0, tiled=True
    ).astype(jnp.float32)
    swap = [(0, 1), (1, 0)]
    partner = lax.ppermute(arrived, "hc", swap)

    def expert_part(rows):
        gate_values = jnp.einsum(
            "pjd,df->pjf", rows, expert_gate[0], preferred_element_type=jnp.float32
        )
        upward = jnp.einsum("pjd,df->pjf", rows, expert_up[0], preferred_element_type=jnp.float32)
        activation = (jax.nn.silu(gate_values) * upward).astype(jnp.bfloat16)
        return jnp.einsum(
            "pjf,fd->pjd", activation, expert_down[0], preferred_element_type=jnp.float32
        )

    own_part = expert_part(arrived)
    partner_part = expert_part(partner)
    partner_back = lax.ppermute(partner_part.astype(jnp.bfloat16), "hc", swap)
    expert_done = (own_part + partner_back.astype(jnp.float32)).astype(jnp.bfloat16)
    returned = lax.all_to_all(expert_done, chips, split_axis=0, concat_axis=0, tiled=True)
    combine = jnp.sum(jnp.where(hit, route_weight[:, :, None, None], 0.0), axis=1)
    routed = jnp.einsum(
        "tpj,pjd->td",
        combine,
        returned.astype(jnp.float32),
        precision=lax.Precision.HIGHEST,
        preferred_element_type=jnp.float32,
    )
    return (residual_own.astype(jnp.float32) + shared_own + routed).astype(jnp.bfloat16)


def solution(mesh):
    core_count = 2
    split_mesh = jax.sharding.Mesh(
        mesh.devices.reshape(
            mesh.shape["req"], mesh.shape["head"] // core_count, core_count
        ),
        ("req", "hx", "hc"),
    )
    head = ("hx", "hc")
    every = ("req", "hx", "hc")
    in_specs = (
        P("req", None),
        P("req", None, None),
        P("req", None, None),
        P("req"),
        P(),
        P(None, head),
        P(),
        P(),
        P(),
        P(None, head),
        P(None, head),
        P(head, None),
        P(),
        P(),
        P(every, None),
        P(None, head),
        P(None, head),
        P(head, None),
        P(every, None, None),
        P(every, None, None),
        P(every, None, None),
    )
    out_specs = P(every, None)
    return jax.shard_map(
        per_device, mesh=split_mesh, in_specs=in_specs, out_specs=out_specs, check_vma=False
    )
```

```python
import math

import jax
import jax.numpy as jnp
from jax import lax
from jax.sharding import PartitionSpec as P

NOPE = 128
ROPE = 64
VDIM = 128
LATENT = 512
EXPERTS = 64
CAP = 14


def rms_scale(values, gain_row):
    return values * lax.rsqrt(jnp.mean(values * values, axis=-1, keepdims=True) + 1e-06) * gain_row


def rotate(values, positions):
    half_size = values.shape[-1] // 2
    frequency = jnp.exp(
        jnp.arange(half_size, dtype=jnp.float32) * (-2.0 * math.log(10000.0) / values.shape[-1])
    )
    angles = positions.astype(jnp.float32)[:, None] * frequency[None, :]
    shape_mid = (angles.shape[0],) + (1,) * (values.ndim - 2) + (half_size,)
    cosine = jnp.cos(angles).reshape(shape_mid)
    sine_part = jnp.sin(angles).reshape(shape_mid)
    first_half = values[..., :half_size]
    second_half = values[..., half_size:]
    return jnp.concatenate(
        [
            first_half * cosine - second_half * sine_part,
            second_half * cosine + first_half * sine_part,
        ],
        axis=-1,
    )


def attend_rows(absorbed, query_rope, first_row, cache_lat, cache_keys, length, new_latent, new_rope):
    query_count = absorbed.shape[0]
    cache_rows = cache_lat.shape[0]
    score_scale = (NOPE + ROPE) ** (-0.5)
    seen_new = first_row + query_count
    keys_latent = jnp.concatenate([cache_lat, new_latent[:seen_new]], axis=0)
    keys_rope = jnp.concatenate([cache_keys, new_rope[:seen_new]], axis=0)
    scores = (
        jnp.einsum("qhl,kl->qhk", absorbed, keys_latent, preferred_element_type=jnp.float32)
        + jnp.einsum("qhr,kr->qhk", query_rope, keys_rope, preferred_element_type=jnp.float32)
    ) * score_scale
    key_index = jnp.arange(cache_rows + seen_new, dtype=jnp.int32)[None, :]
    query_pos = first_row + jnp.arange(query_count, dtype=jnp.int32)[:, None]
    visible = jnp.where(
        key_index < cache_rows, key_index < length, key_index - cache_rows <= query_pos
    )
    scores = jnp.where(visible[:, None, :], scores, -jnp.inf)
    row_max = jnp.max(scores, axis=-1)
    exponent = jnp.exp(scores - row_max[..., None])
    row_total = jnp.sum(exponent, axis=-1)
    weighted = jnp.einsum(
        "qhk,kl->qhl",
        exponent.astype(jnp.bfloat16),
        keys_latent,
        preferred_element_type=jnp.float32,
    )
    return (weighted / row_total[..., None]).astype(jnp.bfloat16)


def per_device(
    hidden_in,
    cache_latent,
    cache_rope,
    cache_lengths,
    attn_gain,
    w_query,
    w_latent,
    w_latent_rope,
    latent_gain,
    w_key_up,
    w_value_up,
    w_out,
    post_gain,
    w_router,
    routes,
    shared_gate,
    shared_up,
    shared_down,
    expert_gate,
    expert_up,
    expert_down,
):
    request_rows = hidden_in.shape[0]
    model_width = hidden_in.shape[1]
    row_count = routes.shape[0]
    top_count = routes.shape[1]
    head_local = w_query.shape[1] // (NOPE + ROPE)
    length = cache_lengths[0]
    chip_count = lax.axis_size("hx")
    core_count = lax.axis_size("hc")
    chip_index = lax.axis_index("hx")
    core_index = lax.axis_index("hc")
    normed_in = rms_scale(hidden_in.astype(jnp.float32), attn_gain).astype(jnp.bfloat16)
    positions = length + jnp.arange(request_rows, dtype=jnp.int32)
    query_all = jnp.dot(normed_in, w_query, preferred_element_type=jnp.float32).reshape(
        request_rows, head_local, NOPE + ROPE
    )
    query_nope = query_all[..., :NOPE].astype(jnp.bfloat16)
    query_rope = rotate(query_all[..., NOPE:], positions).astype(jnp.bfloat16)
    new_latent = rms_scale(
        jnp.dot(normed_in, w_latent, preferred_element_type=jnp.float32), latent_gain
    ).astype(jnp.bfloat16)
    new_rope = rotate(
        jnp.dot(normed_in, w_latent_rope, preferred_element_type=jnp.float32), positions
    ).astype(jnp.bfloat16)
    key_up = w_key_up.reshape(LATENT, head_local, NOPE)
    absorbed = jnp.einsum(
        "chn,lhn->chl", query_nope, key_up, preferred_element_type=jnp.float32
    ).astype(jnp.bfloat16)
    value_up = w_value_up.reshape(LATENT, head_local, VDIM)
    block_rows = min(512, request_rows)
    outputs = []
    for first_row in range(0, request_rows, block_rows):
        latent_out = attend_rows(
            absorbed[first_row : first_row + block_rows],
            query_rope[first_row : first_row + block_rows],
            first_row,
            cache_latent[0],
            cache_rope[0],
            length,
            new_latent,
            new_rope,
        )
        head_out = jnp.einsum(
            "qhl,lhv->qhv", latent_out, value_up, preferred_element_type=jnp.float32
        ).astype(jnp.bfloat16)
        outputs.append(head_out.reshape(block_rows, head_local * VDIM))
    head_rows = jnp.concatenate(outputs, axis=0)
    head_count = chip_count * core_count
    head_index = chip_index * core_count + core_index
    attn_term = jnp.dot(head_rows, w_out, preferred_element_type=jnp.float32).astype(jnp.bfloat16)
    attn_blocks = attn_term.reshape(chip_count, core_count, row_count, model_width)
    keep = lax.dynamic_index_in_dim(attn_blocks, core_index, axis=1, keepdims=False)
    give = lax.dynamic_index_in_dim(attn_blocks, 1 - core_index, axis=1, keepdims=False)
    given = lax.ppermute(give, "hc", [(0, 1), (1, 0)])
    attn_chip = (keep.astype(jnp.float32) + given.astype(jnp.float32)).astype(jnp.bfloat16)
    attn_parts = lax.all_to_all(attn_chip, "hx", split_axis=0, concat_axis=0, tiled=True)
    attn_own = jnp.sum(attn_parts.astype(jnp.float32), axis=0)
    own_start = head_index * row_count
    hidden_own = lax.dynamic_slice_in_dim(hidden_in, own_start, row_count, 0)
    residual_own = (hidden_own.astype(jnp.float32) + attn_own).astype(jnp.bfloat16)
    normed_own = rms_scale(residual_own.astype(jnp.float32), post_gain).astype(jnp.bfloat16)
    normed_all = lax.all_gather(normed_own, ("hx", "hc"), axis=0, tiled=True)
    experts = EXPERTS
    capacity = CAP
    logits = jnp.dot(normed_own, w_router, preferred_element_type=jnp.float32)
    matches = routes[:, :, None] == jnp.arange(experts, dtype=jnp.int32)[None, None, :]
    chosen = jnp.sum(jnp.where(matches, logits[:, None, :], 0.0), axis=-1)
    route_weight = jax.nn.softmax(chosen, axis=-1)
    pair_hits = matches.reshape(row_count * top_count, experts).astype(jnp.int32)
    pair_ranks = jnp.cumsum(pair_hits, axis=0) - pair_hits
    slot_of = jnp.sum(pair_ranks * pair_hits, axis=-1)
    slot_width = -(-capacity // 16) * 16
    target = (routes.reshape(-1) * slot_width + slot_of).reshape(row_count, top_count)
    chips = ("req", "hx")
    chip_total = lax.axis_size(chips)
    dest_ids = jnp.arange(chip_total, dtype=jnp.int32)[:, None] * slot_width + jnp.arange(
        slot_width, dtype=jnp.int32
    )[None, :]
    hit = target[:, :, None, None] == dest_ids[None, None, :, :]
    dispatch = jnp.any(hit, axis=1).astype(jnp.bfloat16)
    outgoing = jnp.einsum(
        "tpj,td->pjd", dispatch, normed_own, preferred_element_type=jnp.float32
    ).astype(jnp.bfloat16)
    arrived = lax.all_to_all(outgoing, chips, split_axis=0, concat_axis=0, tiled=True)
    normed_all, arrived = lax.optimization_barrier((normed_all, arrived))
    normed = (
        normed_all.reshape(chip_count, core_count, row_count, model_width)
        .transpose(1, 0, 2, 3)
        .reshape(request_rows, model_width)
    )
    shared_act = (
        jax.nn.silu(jnp.dot(normed, shared_gate, preferred_element_type=jnp.float32))
        * jnp.dot(normed, shared_up, preferred_element_type=jnp.float32)
    ).astype(jnp.bfloat16)
    shared_part = jnp.dot(shared_act, shared_down, preferred_element_type=jnp.float32)
    shared_core = lax.psum_scatter(shared_part, "hc", scatter_dimension=0, tiled=True)
    shared_own = lax.psum_scatter(
        shared_core.astype(jnp.bfloat16), "hx", scatter_dimension=0, tiled=True
    ).astype(jnp.float32)
    swap = [(0, 1), (1, 0)]
    partner = lax.ppermute(arrived, "hc", swap)

    def expert_part(rows):
        gate_values = jnp.einsum(
            "pjd,df->pjf", rows, expert_gate[0], preferred_element_type=jnp.float32
        )
        upward = jnp.einsum("pjd,df->pjf", rows, expert_up[0], preferred_element_type=jnp.float32)
        activation = (jax.nn.silu(gate_values) * upward).astype(jnp.bfloat16)
        return jnp.einsum(
            "pjf,fd->pjd", activation, expert_down[0], preferred_element_type=jnp.float32
        )

    own_part = expert_part(arrived)
    partner_part = expert_part(partner)
    partner_back = lax.ppermute(partner_part.astype(jnp.bfloat16), "hc", swap)
    expert_done = (own_part + partner_back.astype(jnp.float32)).astype(jnp.bfloat16)
    returned = lax.all_to_all(expert_done, chips, split_axis=0, concat_axis=0, tiled=True)
    combine = jnp.sum(jnp.where(hit, route_weight[:, :, None, None], 0.0), axis=1)
    routed = jnp.einsum(
        "tpj,pjd->td",
        combine,
        returned.astype(jnp.float32),
        precision=lax.Precision.HIGHEST,
        preferred_element_type=jnp.float32,
    )
    return (residual_own.astype(jnp.float32) + shared_own + routed).astype(jnp.bfloat16)


def solution(mesh):
    core_count = 2
    split_mesh = jax.sharding.Mesh(
        mesh.devices.reshape(
            mesh.shape["req"], mesh.shape["head"] // core_count, core_count
        ),
        ("req", "hx", "hc"),
    )
    head = ("hx", "hc")
    every = ("req", "hx", "hc")
    in_specs = (
        P("req", None),
        P("req", None, None),
        P("req", None, None),
        P("req"),
        P(),
        P(None, head),
        P(),
        P(),
        P(),
        P(None, head),
        P(None, head),
        P(head, None),
        P(),
        P(),
        P(every, None),
        P(None, head),
        P(None, head),
        P(head, None),
        P(every, None, None),
        P(every, None, None),
        P(every, None, None),
    )
    out_specs = P(every, None)
    return jax.shard_map(
        per_device, mesh=split_mesh, in_specs=in_specs, out_specs=out_specs, check_vma=False
    )
```

```python
import math

import jax
import jax.numpy as jnp
from jax import lax
from jax.sharding import PartitionSpec as P

NOPE = 128
ROPE = 64
VDIM = 128
LATENT = 512
EXPERTS = 64
CAP = 14


def rms_scale(values, gain_row):
    return values * lax.rsqrt(jnp.mean(values * values, axis=-1, keepdims=True) + 1e-06) * gain_row


def rotate(values, positions):
    half_size = values.shape[-1] // 2
    frequency = jnp.exp(
        jnp.arange(half_size, dtype=jnp.float32) * (-2.0 * math.log(10000.0) / values.shape[-1])
    )
    angles = positions.astype(jnp.float32)[:, None] * frequency[None, :]
    shape_mid = (angles.shape[0],) + (1,) * (values.ndim - 2) + (half_size,)
    cosine = jnp.cos(angles).reshape(shape_mid)
    sine_part = jnp.sin(angles).reshape(shape_mid)
    first_half = values[..., :half_size]
    second_half = values[..., half_size:]
    return jnp.concatenate(
        [
            first_half * cosine - second_half * sine_part,
            second_half * cosine + first_half * sine_part,
        ],
        axis=-1,
    )


def attend_rows(absorbed, query_rope, first_row, cache_lat, cache_keys, length, new_latent, new_rope):
    query_count = absorbed.shape[0]
    cache_rows = cache_lat.shape[0]
    score_scale = (NOPE + ROPE) ** (-0.5)
    seen_new = first_row + query_count
    keys_latent = jnp.concatenate([cache_lat, new_latent[:seen_new]], axis=0)
    keys_rope = jnp.concatenate([cache_keys, new_rope[:seen_new]], axis=0)
    scores = (
        jnp.einsum("qhl,kl->qhk", absorbed, keys_latent, preferred_element_type=jnp.float32)
        + jnp.einsum("qhr,kr->qhk", query_rope, keys_rope, preferred_element_type=jnp.float32)
    ) * score_scale
    key_index = jnp.arange(cache_rows + seen_new, dtype=jnp.int32)[None, :]
    query_pos = first_row + jnp.arange(query_count, dtype=jnp.int32)[:, None]
    visible = jnp.where(
        key_index < cache_rows, key_index < length, key_index - cache_rows <= query_pos
    )
    scores = jnp.where(visible[:, None, :], scores, -jnp.inf)
    row_max = jnp.max(scores, axis=-1)
    exponent = jnp.exp(scores - row_max[..., None])
    row_total = jnp.sum(exponent, axis=-1)
    weighted = jnp.einsum(
        "qhk,kl->qhl",
        exponent.astype(jnp.bfloat16),
        keys_latent,
        preferred_element_type=jnp.float32,
    )
    return (weighted / row_total[..., None]).astype(jnp.bfloat16)


def per_device(
    hidden_in,
    cache_latent,
    cache_rope,
    cache_lengths,
    attn_gain,
    w_query,
    w_latent,
    w_latent_rope,
    latent_gain,
    w_key_up,
    w_value_up,
    w_out,
    post_gain,
    w_router,
    routes,
    shared_gate,
    shared_up,
    shared_down,
    expert_gate,
    expert_up,
    expert_down,
):
    request_rows = hidden_in.shape[0]
    model_width = hidden_in.shape[1]
    row_count = routes.shape[0]
    top_count = routes.shape[1]
    head_local = w_query.shape[1] // (NOPE + ROPE)
    length = cache_lengths[0]
    chip_count = lax.axis_size("hx")
    core_count = lax.axis_size("hc")
    chip_index = lax.axis_index("hx")
    core_index = lax.axis_index("hc")
    normed_in = rms_scale(hidden_in.astype(jnp.float32), attn_gain).astype(jnp.bfloat16)
    positions = length + jnp.arange(request_rows, dtype=jnp.int32)
    query_all = jnp.dot(normed_in, w_query, preferred_element_type=jnp.float32).reshape(
        request_rows, head_local, NOPE + ROPE
    )
    query_nope = query_all[..., :NOPE].astype(jnp.bfloat16)
    query_rope = rotate(query_all[..., NOPE:], positions).astype(jnp.bfloat16)
    new_latent = rms_scale(
        jnp.dot(normed_in, w_latent, preferred_element_type=jnp.float32), latent_gain
    ).astype(jnp.bfloat16)
    new_rope = rotate(
        jnp.dot(normed_in, w_latent_rope, preferred_element_type=jnp.float32), positions
    ).astype(jnp.bfloat16)
    key_up = w_key_up.reshape(LATENT, head_local, NOPE)
    absorbed = jnp.einsum(
        "chn,lhn->chl", query_nope, key_up, preferred_element_type=jnp.float32
    ).astype(jnp.bfloat16)
    value_up = w_value_up.reshape(LATENT, head_local, VDIM)
    block_rows = min(512, request_rows)
    outputs = []
    for first_row in range(0, request_rows, block_rows):
        latent_out = attend_rows(
            absorbed[first_row : first_row + block_rows],
            query_rope[first_row : first_row + block_rows],
            first_row,
            cache_latent[0],
            cache_rope[0],
            length,
            new_latent,
            new_rope,
        )
        head_out = jnp.einsum(
            "qhl,lhv->qhv", latent_out, value_up, preferred_element_type=jnp.float32
        ).astype(jnp.bfloat16)
        outputs.append(head_out.reshape(block_rows, head_local * VDIM))
    head_rows = jnp.concatenate(outputs, axis=0)
    head_count = chip_count * core_count
    head_index = chip_index * core_count + core_index
    attn_term = jnp.dot(head_rows, w_out, preferred_element_type=jnp.float32).astype(jnp.bfloat16)
    attn_blocks = attn_term.reshape(chip_count, core_count, row_count, model_width)
    keep = lax.dynamic_index_in_dim(attn_blocks, core_index, axis=1, keepdims=False)
    give = lax.dynamic_index_in_dim(attn_blocks, 1 - core_index, axis=1, keepdims=False)
    given = lax.ppermute(give, "hc", [(0, 1), (1, 0)])
    attn_chip = (keep.astype(jnp.float32) + given.astype(jnp.float32)).astype(jnp.bfloat16)
    attn_parts = lax.all_to_all(attn_chip, "hx", split_axis=0, concat_axis=0, tiled=True)
    attn_own = jnp.sum(attn_parts.astype(jnp.float32), axis=0)
    own_start = head_index * row_count
    hidden_own = lax.dynamic_slice_in_dim(hidden_in, own_start, row_count, 0)
    residual_own = (hidden_own.astype(jnp.float32) + attn_own).astype(jnp.bfloat16)
    normed_own = rms_scale(residual_own.astype(jnp.float32), post_gain).astype(jnp.bfloat16)
    normed_all = lax.all_gather(normed_own, ("hx", "hc"), axis=0, tiled=True)
    experts = EXPERTS
    capacity = CAP
    logits = jnp.dot(normed_own, w_router, preferred_element_type=jnp.float32)
    matches = routes[:, :, None] == jnp.arange(experts, dtype=jnp.int32)[None, None, :]
    chosen = jnp.sum(jnp.where(matches, logits[:, None, :], 0.0), axis=-1)
    route_weight = jax.nn.softmax(chosen, axis=-1)
    pair_hits = matches.reshape(row_count * top_count, experts).astype(jnp.int32)
    pair_ranks = jnp.cumsum(pair_hits, axis=0) - pair_hits
    slot_of = jnp.sum(pair_ranks * pair_hits, axis=-1)
    slot_width = -(-capacity // 16) * 16
    target = (routes.reshape(-1) * slot_width + slot_of).reshape(row_count, top_count)
    chips = ("req", "hx")
    chip_total = lax.axis_size(chips)
    dest_ids = jnp.arange(chip_total, dtype=jnp.int32)[:, None] * slot_width + jnp.arange(
        slot_width, dtype=jnp.int32
    )[None, :]
    hit = target[:, :, None, None] == dest_ids[None, None, :, :]
    dispatch = jnp.any(hit, axis=1).astype(jnp.bfloat16)
    outgoing = jnp.einsum(
        "tpj,td->pjd", dispatch, normed_own, preferred_element_type=jnp.float32
    ).astype(jnp.bfloat16)
    arrived = lax.all_to_all(outgoing, chips, split_axis=0, concat_axis=0, tiled=True).reshape(
        chip_total * slot_width, model_width
    )
    normed_all, arrived = lax.optimization_barrier((normed_all, arrived))
    normed = (
        normed_all.reshape(chip_count, core_count, row_count, model_width)
        .transpose(1, 0, 2, 3)
        .reshape(request_rows, model_width)
    )
    shared_act = (
        jax.nn.silu(jnp.dot(normed, shared_gate, preferred_element_type=jnp.float32))
        * jnp.dot(normed, shared_up, preferred_element_type=jnp.float32)
    ).astype(jnp.bfloat16)
    shared_part = jnp.dot(shared_act, shared_down, preferred_element_type=jnp.float32)
    shared_core = lax.psum_scatter(shared_part, "hc", scatter_dimension=0, tiled=True)
    shared_own = lax.psum_scatter(
        shared_core.astype(jnp.bfloat16), "hx", scatter_dimension=0, tiled=True
    ).astype(jnp.float32)
    swap = [(0, 1), (1, 0)]
    partner = lax.ppermute(arrived, "hc", swap)

    def expert_part(rows):
        gate_values = jnp.dot(rows, expert_gate[0], preferred_element_type=jnp.float32)
        upward = jnp.dot(rows, expert_up[0], preferred_element_type=jnp.float32)
        activation = (jax.nn.silu(gate_values) * upward).astype(jnp.bfloat16)
        return jnp.dot(activation, expert_down[0], preferred_element_type=jnp.float32)

    own_part = expert_part(arrived)
    partner_part = expert_part(partner)
    partner_back = lax.ppermute(partner_part.astype(jnp.bfloat16), "hc", swap)
    expert_done = (own_part + partner_back.astype(jnp.float32)).astype(jnp.bfloat16)
    returned = lax.all_to_all(
        expert_done.reshape(chip_total, slot_width, model_width),
        chips,
        split_axis=0,
        concat_axis=0,
        tiled=True,
    )
    combine = jnp.sum(jnp.where(hit, route_weight[:, :, None, None], 0.0), axis=1)
    routed = jnp.einsum(
        "tpj,pjd->td",
        combine,
        returned.astype(jnp.float32),
        precision=lax.Precision.HIGHEST,
        preferred_element_type=jnp.float32,
    )
    return (residual_own.astype(jnp.float32) + shared_own + routed).astype(jnp.bfloat16)


def solution(mesh):
    core_count = 2
    split_mesh = jax.sharding.Mesh(
        mesh.devices.reshape(
            mesh.shape["req"], mesh.shape["head"] // core_count, core_count
        ),
        ("req", "hx", "hc"),
    )
    head = ("hx", "hc")
    every = ("req", "hx", "hc")
    in_specs = (
        P("req", None),
        P("req", None, None),
        P("req", None, None),
        P("req"),
        P(),
        P(None, head),
        P(),
        P(),
        P(),
        P(None, head),
        P(None, head),
        P(head, None),
        P(),
        P(),
        P(every, None),
        P(None, head),
        P(None, head),
        P(head, None),
        P(every, None, None),
        P(every, None, None),
        P(every, None, None),
    )
    out_specs = P(every, None)
    return jax.shard_map(
        per_device, mesh=split_mesh, in_specs=in_specs, out_specs=out_specs, check_vma=False
    )
```

```python
import math

import jax
import jax.numpy as jnp
from jax import lax
from jax.sharding import PartitionSpec as P

NOPE = 128
ROPE = 64
VDIM = 128
LATENT = 512
EXPERTS = 64
CAP = 14


def rms_scale(values, gain_row):
    return values * lax.rsqrt(jnp.mean(values * values, axis=-1, keepdims=True) + 1e-06) * gain_row


def rotate(values, positions):
    half_size = values.shape[-1] // 2
    frequency = jnp.exp(
        jnp.arange(half_size, dtype=jnp.float32) * (-2.0 * math.log(10000.0) / values.shape[-1])
    )
    angles = positions.astype(jnp.float32)[:, None] * frequency[None, :]
    shape_mid = (angles.shape[0],) + (1,) * (values.ndim - 2) + (half_size,)
    cosine = jnp.cos(angles).reshape(shape_mid)
    sine_part = jnp.sin(angles).reshape(shape_mid)
    first_half = values[..., :half_size]
    second_half = values[..., half_size:]
    return jnp.concatenate(
        [
            first_half * cosine - second_half * sine_part,
            second_half * cosine + first_half * sine_part,
        ],
        axis=-1,
    )


def attend_rows(absorbed, query_rope, first_row, cache_lat, cache_keys, length, new_latent, new_rope):
    query_count = absorbed.shape[0]
    cache_rows = cache_lat.shape[0]
    score_scale = (NOPE + ROPE) ** (-0.5)
    seen_new = first_row + query_count
    keys_latent = jnp.concatenate([cache_lat, new_latent[:seen_new]], axis=0)
    keys_rope = jnp.concatenate([cache_keys, new_rope[:seen_new]], axis=0)
    scores = (
        jnp.einsum("qhl,kl->qhk", absorbed, keys_latent, preferred_element_type=jnp.float32)
        + jnp.einsum("qhr,kr->qhk", query_rope, keys_rope, preferred_element_type=jnp.float32)
    ) * score_scale
    key_index = jnp.arange(cache_rows + seen_new, dtype=jnp.int32)[None, :]
    query_pos = first_row + jnp.arange(query_count, dtype=jnp.int32)[:, None]
    visible = jnp.where(
        key_index < cache_rows, key_index < length, key_index - cache_rows <= query_pos
    )
    scores = jnp.where(visible[:, None, :], scores, -jnp.inf)
    row_max = jnp.max(scores, axis=-1)
    exponent = jnp.exp(scores - row_max[..., None])
    row_total = jnp.sum(exponent, axis=-1)
    weighted = jnp.einsum(
        "qhk,kl->qhl",
        exponent.astype(jnp.bfloat16),
        keys_latent,
        preferred_element_type=jnp.float32,
    )
    return (weighted / row_total[..., None]).astype(jnp.bfloat16)


def per_device(
    hidden_in,
    cache_latent,
    cache_rope,
    cache_lengths,
    attn_gain,
    w_query,
    w_latent,
    w_latent_rope,
    latent_gain,
    w_key_up,
    w_value_up,
    w_out,
    post_gain,
    w_router,
    routes,
    shared_gate,
    shared_up,
    shared_down,
    expert_gate,
    expert_up,
    expert_down,
):
    request_rows = hidden_in.shape[0]
    model_width = hidden_in.shape[1]
    row_count = routes.shape[0]
    top_count = routes.shape[1]
    head_local = w_query.shape[1] // (NOPE + ROPE)
    length = cache_lengths[0]
    chip_count = lax.axis_size("hx")
    core_count = lax.axis_size("hc")
    chip_index = lax.axis_index("hx")
    core_index = lax.axis_index("hc")
    normed_in = rms_scale(hidden_in.astype(jnp.float32), attn_gain).astype(jnp.bfloat16)
    positions = length + jnp.arange(request_rows, dtype=jnp.int32)
    query_all = jnp.dot(normed_in, w_query, preferred_element_type=jnp.float32).reshape(
        request_rows, head_local, NOPE + ROPE
    )
    query_nope = query_all[..., :NOPE].astype(jnp.bfloat16)
    query_rope = rotate(query_all[..., NOPE:], positions).astype(jnp.bfloat16)
    new_latent = rms_scale(
        jnp.dot(normed_in, w_latent, preferred_element_type=jnp.float32), latent_gain
    ).astype(jnp.bfloat16)
    new_rope = rotate(
        jnp.dot(normed_in, w_latent_rope, preferred_element_type=jnp.float32), positions
    ).astype(jnp.bfloat16)
    key_up = w_key_up.reshape(LATENT, head_local, NOPE)
    absorbed = jnp.einsum(
        "chn,lhn->chl", query_nope, key_up, preferred_element_type=jnp.float32
    ).astype(jnp.bfloat16)
    value_up = w_value_up.reshape(LATENT, head_local, VDIM)
    block_rows = min(256, request_rows)
    outputs = []
    for first_row in range(0, request_rows, block_rows):
        latent_out = attend_rows(
            absorbed[first_row : first_row + block_rows],
            query_rope[first_row : first_row + block_rows],
            first_row,
            cache_latent[0],
            cache_rope[0],
            length,
            new_latent,
            new_rope,
        )
        head_out = jnp.einsum(
            "qhl,lhv->qhv", latent_out, value_up, preferred_element_type=jnp.float32
        ).astype(jnp.bfloat16)
        outputs.append(head_out.reshape(block_rows, head_local * VDIM))
    head_rows = jnp.concatenate(outputs, axis=0)
    head_count = chip_count * core_count
    head_index = chip_index * core_count + core_index
    attn_term = jnp.dot(head_rows, w_out, preferred_element_type=jnp.float32).astype(jnp.bfloat16)
    attn_blocks = attn_term.reshape(chip_count, core_count, row_count, model_width)
    keep = lax.dynamic_index_in_dim(attn_blocks, core_index, axis=1, keepdims=False)
    give = lax.dynamic_index_in_dim(attn_blocks, 1 - core_index, axis=1, keepdims=False)
    given = lax.ppermute(give, "hc", [(0, 1), (1, 0)])
    attn_chip = (keep.astype(jnp.float32) + given.astype(jnp.float32)).astype(jnp.bfloat16)
    attn_parts = lax.all_to_all(attn_chip, "hx", split_axis=0, concat_axis=0, tiled=True)
    attn_own = jnp.sum(attn_parts.astype(jnp.float32), axis=0)
    own_start = head_index * row_count
    hidden_own = lax.dynamic_slice_in_dim(hidden_in, own_start, row_count, 0)
    residual_own = (hidden_own.astype(jnp.float32) + attn_own).astype(jnp.bfloat16)
    normed_own = rms_scale(residual_own.astype(jnp.float32), post_gain).astype(jnp.bfloat16)
    normed_all = lax.all_gather(normed_own, ("hx", "hc"), axis=0, tiled=True)
    experts = EXPERTS
    capacity = CAP
    logits = jnp.dot(normed_own, w_router, preferred_element_type=jnp.float32)
    matches = routes[:, :, None] == jnp.arange(experts, dtype=jnp.int32)[None, None, :]
    chosen = jnp.sum(jnp.where(matches, logits[:, None, :], 0.0), axis=-1)
    route_weight = jax.nn.softmax(chosen, axis=-1)
    pair_hits = matches.reshape(row_count * top_count, experts).astype(jnp.int32)
    pair_ranks = jnp.cumsum(pair_hits, axis=0) - pair_hits
    slot_of = jnp.sum(pair_ranks * pair_hits, axis=-1)
    slot_width = -(-capacity // 16) * 16
    target = (routes.reshape(-1) * slot_width + slot_of).reshape(row_count, top_count)
    chips = ("req", "hx")
    chip_total = lax.axis_size(chips)
    dest_ids = jnp.arange(chip_total, dtype=jnp.int32)[:, None] * slot_width + jnp.arange(
        slot_width, dtype=jnp.int32
    )[None, :]
    hit = target[:, :, None, None] == dest_ids[None, None, :, :]
    dispatch = jnp.any(hit, axis=1).astype(jnp.bfloat16)
    outgoing = jnp.einsum(
        "tpj,td->pjd", dispatch, normed_own, preferred_element_type=jnp.float32
    ).astype(jnp.bfloat16)
    arrived = lax.all_to_all(outgoing, chips, split_axis=0, concat_axis=0, tiled=True)
    normed_all, arrived = lax.optimization_barrier((normed_all, arrived))
    normed = (
        normed_all.reshape(chip_count, core_count, row_count, model_width)
        .transpose(1, 0, 2, 3)
        .reshape(request_rows, model_width)
    )
    shared_act = (
        jax.nn.silu(jnp.dot(normed, shared_gate, preferred_element_type=jnp.float32))
        * jnp.dot(normed, shared_up, preferred_element_type=jnp.float32)
    ).astype(jnp.bfloat16)
    shared_part = jnp.dot(shared_act, shared_down, preferred_element_type=jnp.float32)
    shared_core = lax.psum_scatter(shared_part, "hc", scatter_dimension=0, tiled=True)
    shared_own = lax.psum_scatter(
        shared_core.astype(jnp.bfloat16), "hx", scatter_dimension=0, tiled=True
    ).astype(jnp.float32)
    swap = [(0, 1), (1, 0)]
    partner = lax.ppermute(arrived, "hc", swap)

    def expert_part(rows):
        gate_values = jnp.einsum(
            "pjd,df->pjf", rows, expert_gate[0], preferred_element_type=jnp.float32
        )
        upward = jnp.einsum("pjd,df->pjf", rows, expert_up[0], preferred_element_type=jnp.float32)
        activation = (jax.nn.silu(gate_values) * upward).astype(jnp.bfloat16)
        return jnp.einsum(
            "pjf,fd->pjd", activation, expert_down[0], preferred_element_type=jnp.float32
        )

    own_part = expert_part(arrived)
    partner_part = expert_part(partner)
    partner_back = lax.ppermute(partner_part.astype(jnp.bfloat16), "hc", swap)
    expert_done = (own_part + partner_back.astype(jnp.float32)).astype(jnp.bfloat16)
    returned = lax.all_to_all(expert_done, chips, split_axis=0, concat_axis=0, tiled=True)
    combine = jnp.sum(jnp.where(hit, route_weight[:, :, None, None], 0.0), axis=1)
    routed = jnp.einsum(
        "tpj,pjd->td",
        combine,
        returned.astype(jnp.float32),
        precision=lax.Precision.HIGHEST,
        preferred_element_type=jnp.float32,
    )
    return (residual_own.astype(jnp.float32) + shared_own + routed).astype(jnp.bfloat16)


def solution(mesh):
    core_count = 2
    split_mesh = jax.sharding.Mesh(
        mesh.devices.reshape(
            mesh.shape["req"], mesh.shape["head"] // core_count, core_count
        ),
        ("req", "hx", "hc"),
    )
    head = ("hx", "hc")
    every = ("req", "hx", "hc")
    in_specs = (
        P("req", None),
        P("req", None, None),
        P("req", None, None),
        P("req"),
        P(),
        P(None, head),
        P(),
        P(),
        P(),
        P(None, head),
        P(None, head),
        P(head, None),
        P(),
        P(),
        P(every, None),
        P(None, head),
        P(None, head),
        P(head, None),
        P(every, None, None),
        P(every, None, None),
        P(every, None, None),
    )
    out_specs = P(every, None)
    return jax.shard_map(
        per_device, mesh=split_mesh, in_specs=in_specs, out_specs=out_specs, check_vma=False
    )
```

```python
import math

import jax
import jax.numpy as jnp
from jax import lax
from jax.sharding import PartitionSpec as P

NOPE = 128
ROPE = 64
VDIM = 128
LATENT = 512
EXPERTS = 64
CAP = 14


def rms_scale(values, gain_row):
    return values * lax.rsqrt(jnp.mean(values * values, axis=-1, keepdims=True) + 1e-06) * gain_row


def rotate(values, positions):
    half_size = values.shape[-1] // 2
    frequency = jnp.exp(
        jnp.arange(half_size, dtype=jnp.float32) * (-2.0 * math.log(10000.0) / values.shape[-1])
    )
    angles = positions.astype(jnp.float32)[:, None] * frequency[None, :]
    shape_mid = (angles.shape[0],) + (1,) * (values.ndim - 2) + (half_size,)
    cosine = jnp.cos(angles).reshape(shape_mid)
    sine_part = jnp.sin(angles).reshape(shape_mid)
    first_half = values[..., :half_size]
    second_half = values[..., half_size:]
    return jnp.concatenate(
        [
            first_half * cosine - second_half * sine_part,
            second_half * cosine + first_half * sine_part,
        ],
        axis=-1,
    )


def attend_rows(absorbed, query_rope, first_row, cache_lat, cache_keys, length, new_latent, new_rope):
    query_count = absorbed.shape[0]
    cache_rows = cache_lat.shape[0]
    score_scale = (NOPE + ROPE) ** (-0.5)
    seen_new = first_row + query_count
    keys_latent = jnp.concatenate([cache_lat, new_latent[:seen_new]], axis=0)
    keys_rope = jnp.concatenate([cache_keys, new_rope[:seen_new]], axis=0)
    scores = (
        jnp.einsum("qhl,kl->qhk", absorbed, keys_latent, preferred_element_type=jnp.float32)
        + jnp.einsum("qhr,kr->qhk", query_rope, keys_rope, preferred_element_type=jnp.float32)
    ) * score_scale
    key_index = jnp.arange(cache_rows + seen_new, dtype=jnp.int32)[None, :]
    query_pos = first_row + jnp.arange(query_count, dtype=jnp.int32)[:, None]
    visible = jnp.where(
        key_index < cache_rows, key_index < length, key_index - cache_rows <= query_pos
    )
    scores = jnp.where(visible[:, None, :], scores, -jnp.inf)
    row_max = jnp.max(scores, axis=-1)
    exponent = jnp.exp(scores - row_max[..., None])
    row_total = jnp.sum(exponent, axis=-1)
    weighted = jnp.einsum(
        "qhk,kl->qhl",
        exponent.astype(jnp.bfloat16),
        keys_latent,
        preferred_element_type=jnp.float32,
    )
    return (weighted / row_total[..., None]).astype(jnp.bfloat16)


def per_device(
    hidden_in,
    cache_latent,
    cache_rope,
    cache_lengths,
    attn_gain,
    w_query,
    w_latent,
    w_latent_rope,
    latent_gain,
    w_key_up,
    w_value_up,
    w_out,
    post_gain,
    w_router,
    routes,
    shared_gate,
    shared_up,
    shared_down,
    expert_gate,
    expert_up,
    expert_down,
):
    request_rows = hidden_in.shape[0]
    model_width = hidden_in.shape[1]
    row_count = routes.shape[0]
    top_count = routes.shape[1]
    head_local = w_query.shape[1] // (NOPE + ROPE)
    length = cache_lengths[0]
    chip_count = lax.axis_size("hx")
    core_count = lax.axis_size("hc")
    chip_index = lax.axis_index("hx")
    core_index = lax.axis_index("hc")
    normed_in = rms_scale(hidden_in.astype(jnp.float32), attn_gain).astype(jnp.bfloat16)
    positions = length + jnp.arange(request_rows, dtype=jnp.int32)
    query_all = jnp.dot(normed_in, w_query, preferred_element_type=jnp.float32).reshape(
        request_rows, head_local, NOPE + ROPE
    )
    query_nope = query_all[..., :NOPE].astype(jnp.bfloat16)
    query_rope = rotate(query_all[..., NOPE:], positions).astype(jnp.bfloat16)
    new_latent = rms_scale(
        jnp.dot(normed_in, w_latent, preferred_element_type=jnp.float32), latent_gain
    ).astype(jnp.bfloat16)
    new_rope = rotate(
        jnp.dot(normed_in, w_latent_rope, preferred_element_type=jnp.float32), positions
    ).astype(jnp.bfloat16)
    key_up = w_key_up.reshape(LATENT, head_local, NOPE)
    absorbed = jnp.einsum(
        "chn,lhn->chl", query_nope, key_up, preferred_element_type=jnp.float32
    ).astype(jnp.bfloat16)
    value_up = w_value_up.reshape(LATENT, head_local, VDIM)
    block_rows = min(512, request_rows)
    outputs = []
    for first_row in range(0, request_rows, block_rows):
        latent_out = attend_rows(
            absorbed[first_row : first_row + block_rows],
            query_rope[first_row : first_row + block_rows],
            first_row,
            cache_latent[0],
            cache_rope[0],
            length,
            new_latent,
            new_rope,
        )
        head_out = jnp.einsum(
            "qhl,lhv->qhv", latent_out, value_up, preferred_element_type=jnp.float32
        ).astype(jnp.bfloat16)
        outputs.append(head_out.reshape(block_rows, head_local * VDIM))
    head_rows = jnp.concatenate(outputs, axis=0)
    head_count = chip_count * core_count
    head_index = chip_index * core_count + core_index
    attn_term = jnp.dot(head_rows, w_out, preferred_element_type=jnp.float32).astype(jnp.bfloat16)
    attn_blocks = attn_term.reshape(chip_count, core_count, row_count, model_width)
    keep = lax.dynamic_index_in_dim(attn_blocks, core_index, axis=1, keepdims=False)
    give = lax.dynamic_index_in_dim(attn_blocks, 1 - core_index, axis=1, keepdims=False)
    given = lax.ppermute(give, "hc", [(0, 1), (1, 0)])
    attn_chip = (keep.astype(jnp.float32) + given.astype(jnp.float32)).astype(jnp.bfloat16)
    attn_parts = lax.all_to_all(attn_chip, "hx", split_axis=0, concat_axis=0, tiled=True)
    attn_own = jnp.sum(attn_parts.astype(jnp.float32), axis=0)
    own_start = head_index * row_count
    hidden_own = lax.dynamic_slice_in_dim(hidden_in, own_start, row_count, 0)
    residual_own = (hidden_own.astype(jnp.float32) + attn_own).astype(jnp.bfloat16)
    normed_own = rms_scale(residual_own.astype(jnp.float32), post_gain).astype(jnp.bfloat16)
    normed_all = lax.all_gather(normed_own, ("hx", "hc"), axis=0, tiled=True)
    swap = [(0, 1), (1, 0)]
    gate_other = lax.ppermute(expert_gate[0], "hc", swap)
    up_other = lax.ppermute(expert_up[0], "hc", swap)
    down_other = lax.ppermute(expert_down[0], "hc", swap)

    gate_other, up_other, down_other, normed_own = lax.optimization_barrier(
        (gate_other, up_other, down_other, normed_own)
    )
    experts = EXPERTS
    capacity = CAP
    logits = jnp.dot(normed_own, w_router, preferred_element_type=jnp.float32)
    matches = routes[:, :, None] == jnp.arange(experts, dtype=jnp.int32)[None, None, :]
    chosen = jnp.sum(jnp.where(matches, logits[:, None, :], 0.0), axis=-1)
    route_weight = jax.nn.softmax(chosen, axis=-1)
    pair_hits = matches.reshape(row_count * top_count, experts).astype(jnp.int32)
    pair_ranks = jnp.cumsum(pair_hits, axis=0) - pair_hits
    slot_of = jnp.sum(pair_ranks * pair_hits, axis=-1)
    slot_width = -(-capacity // 16) * 16
    target = (routes.reshape(-1) * slot_width + slot_of).reshape(row_count, top_count)
    chips = ("req", "hx")
    chip_total = lax.axis_size(chips)
    dest_ids = jnp.arange(chip_total, dtype=jnp.int32)[:, None] * slot_width + jnp.arange(
        slot_width, dtype=jnp.int32
    )[None, :]
    hit = target[:, :, None, None] == dest_ids[None, None, :, :]
    dispatch = jnp.any(hit, axis=1).astype(jnp.bfloat16)
    outgoing = jnp.einsum(
        "tpj,td->pjd", dispatch, normed_own, preferred_element_type=jnp.float32
    ).astype(jnp.bfloat16)
    arrived = lax.all_to_all(outgoing, chips, split_axis=0, concat_axis=0, tiled=True)
    normed_all, arrived = lax.optimization_barrier((normed_all, arrived))
    normed = (
        normed_all.reshape(chip_count, core_count, row_count, model_width)
        .transpose(1, 0, 2, 3)
        .reshape(request_rows, model_width)
    )
    shared_act = (
        jax.nn.silu(jnp.dot(normed, shared_gate, preferred_element_type=jnp.float32))
        * jnp.dot(normed, shared_up, preferred_element_type=jnp.float32)
    ).astype(jnp.bfloat16)
    shared_part = jnp.dot(shared_act, shared_down, preferred_element_type=jnp.float32)
    shared_core = lax.psum_scatter(shared_part, "hc", scatter_dimension=0, tiled=True)
    shared_own = lax.psum_scatter(
        shared_core.astype(jnp.bfloat16), "hx", scatter_dimension=0, tiled=True
    ).astype(jnp.float32)
    def expert_act(rows, gate_w, up_w):
        gate_values = jnp.einsum("pjd,df->pjf", rows, gate_w, preferred_element_type=jnp.float32)
        upward = jnp.einsum("pjd,df->pjf", rows, up_w, preferred_element_type=jnp.float32)
        return (jax.nn.silu(gate_values) * upward).astype(jnp.bfloat16)

    act_own = expert_act(arrived, expert_gate[0], expert_up[0])
    act_other = expert_act(arrived, gate_other, up_other)
    expert_done = (
        jnp.einsum("pjf,fd->pjd", act_own, expert_down[0], preferred_element_type=jnp.float32)
        + jnp.einsum("pjf,fd->pjd", act_other, down_other, preferred_element_type=jnp.float32)
    ).astype(jnp.bfloat16)
    returned = lax.all_to_all(expert_done, chips, split_axis=0, concat_axis=0, tiled=True)
    combine = jnp.sum(jnp.where(hit, route_weight[:, :, None, None], 0.0), axis=1)
    routed = jnp.einsum(
        "tpj,pjd->td",
        combine,
        returned.astype(jnp.float32),
        precision=lax.Precision.HIGHEST,
        preferred_element_type=jnp.float32,
    )
    return (residual_own.astype(jnp.float32) + shared_own + routed).astype(jnp.bfloat16)


def solution(mesh):
    core_count = 2
    split_mesh = jax.sharding.Mesh(
        mesh.devices.reshape(
            mesh.shape["req"], mesh.shape["head"] // core_count, core_count
        ),
        ("req", "hx", "hc"),
    )
    head = ("hx", "hc")
    every = ("req", "hx", "hc")
    in_specs = (
        P("req", None),
        P("req", None, None),
        P("req", None, None),
        P("req"),
        P(),
        P(None, head),
        P(),
        P(),
        P(),
        P(None, head),
        P(None, head),
        P(head, None),
        P(),
        P(),
        P(every, None),
        P(None, head),
        P(None, head),
        P(head, None),
        P(every, None, None),
        P(every, None, None),
        P(every, None, None),
    )
    out_specs = P(every, None)
    return jax.shard_map(
        per_device, mesh=split_mesh, in_specs=in_specs, out_specs=out_specs, check_vma=False
    )
```

```python
import math

import jax
import jax.numpy as jnp
from jax import lax
from jax.sharding import PartitionSpec as P

NOPE = 128
ROPE = 64
VDIM = 128
LATENT = 512
EXPERTS = 64
CAP = 14


def rms_scale(values, gain_row):
    return values * lax.rsqrt(jnp.mean(values * values, axis=-1, keepdims=True) + 1e-06) * gain_row


def rotate(values, positions):
    half_size = values.shape[-1] // 2
    frequency = jnp.exp(
        jnp.arange(half_size, dtype=jnp.float32) * (-2.0 * math.log(10000.0) / values.shape[-1])
    )
    angles = positions.astype(jnp.float32)[:, None] * frequency[None, :]
    shape_mid = (angles.shape[0],) + (1,) * (values.ndim - 2) + (half_size,)
    cosine = jnp.cos(angles).reshape(shape_mid)
    sine_part = jnp.sin(angles).reshape(shape_mid)
    first_half = values[..., :half_size]
    second_half = values[..., half_size:]
    return jnp.concatenate(
        [
            first_half * cosine - second_half * sine_part,
            second_half * cosine + first_half * sine_part,
        ],
        axis=-1,
    )


def attend_rows(absorbed, query_rope, first_row, cache_lat, cache_keys, length, new_latent, new_rope):
    query_count = absorbed.shape[0]
    cache_rows = cache_lat.shape[0]
    score_scale = (NOPE + ROPE) ** (-0.5)
    seen_new = first_row + query_count
    keys_latent = jnp.concatenate([cache_lat, new_latent[:seen_new]], axis=0)
    keys_rope = jnp.concatenate([cache_keys, new_rope[:seen_new]], axis=0)
    scores = (
        jnp.einsum("qhl,kl->qhk", absorbed, keys_latent, preferred_element_type=jnp.float32)
        + jnp.einsum("qhr,kr->qhk", query_rope, keys_rope, preferred_element_type=jnp.float32)
    ) * score_scale
    key_index = jnp.arange(cache_rows + seen_new, dtype=jnp.int32)[None, :]
    query_pos = first_row + jnp.arange(query_count, dtype=jnp.int32)[:, None]
    visible = jnp.where(
        key_index < cache_rows, key_index < length, key_index - cache_rows <= query_pos
    )
    scores = jnp.where(visible[:, None, :], scores, -jnp.inf)
    row_max = jnp.max(scores, axis=-1)
    exponent = jnp.exp(scores - row_max[..., None])
    row_total = jnp.sum(exponent, axis=-1)
    weighted = jnp.einsum(
        "qhk,kl->qhl",
        exponent.astype(jnp.bfloat16),
        keys_latent,
        preferred_element_type=jnp.float32,
    )
    return (weighted / row_total[..., None]).astype(jnp.bfloat16)


def per_device(
    hidden_in,
    cache_latent,
    cache_rope,
    cache_lengths,
    attn_gain,
    w_query,
    w_latent,
    w_latent_rope,
    latent_gain,
    w_key_up,
    w_value_up,
    w_out,
    post_gain,
    w_router,
    routes,
    shared_gate,
    shared_up,
    shared_down,
    expert_gate,
    expert_up,
    expert_down,
):
    request_rows = hidden_in.shape[0]
    model_width = hidden_in.shape[1]
    row_count = routes.shape[0]
    top_count = routes.shape[1]
    head_local = w_query.shape[1] // (NOPE + ROPE)
    length = cache_lengths[0]
    chip_count = lax.axis_size("hx")
    core_count = lax.axis_size("hc")
    chip_index = lax.axis_index("hx")
    core_index = lax.axis_index("hc")
    normed_in = rms_scale(hidden_in.astype(jnp.float32), attn_gain).astype(jnp.bfloat16)
    positions = length + jnp.arange(request_rows, dtype=jnp.int32)
    query_all = jnp.dot(normed_in, w_query, preferred_element_type=jnp.float32).reshape(
        request_rows, head_local, NOPE + ROPE
    )
    query_nope = query_all[..., :NOPE].astype(jnp.bfloat16)
    query_rope = rotate(query_all[..., NOPE:], positions).astype(jnp.bfloat16)
    new_latent = rms_scale(
        jnp.dot(normed_in, w_latent, preferred_element_type=jnp.float32), latent_gain
    ).astype(jnp.bfloat16)
    new_rope = rotate(
        jnp.dot(normed_in, w_latent_rope, preferred_element_type=jnp.float32), positions
    ).astype(jnp.bfloat16)
    key_up = w_key_up.reshape(LATENT, head_local, NOPE)
    absorbed = jnp.einsum(
        "chn,lhn->chl", query_nope, key_up, preferred_element_type=jnp.float32
    ).astype(jnp.bfloat16)
    value_up = w_value_up.reshape(LATENT, head_local, VDIM)
    block_rows = min(512, request_rows)
    outputs = []
    for first_row in range(0, request_rows, block_rows):
        latent_out = attend_rows(
            absorbed[first_row : first_row + block_rows],
            query_rope[first_row : first_row + block_rows],
            first_row,
            cache_latent[0],
            cache_rope[0],
            length,
            new_latent,
            new_rope,
        )
        head_out = jnp.einsum(
            "qhl,lhv->qhv", latent_out, value_up, preferred_element_type=jnp.float32
        ).astype(jnp.bfloat16)
        outputs.append(head_out.reshape(block_rows, head_local * VDIM))
    head_rows = jnp.concatenate(outputs, axis=0)
    head_count = chip_count * core_count
    head_index = chip_index * core_count + core_index
    attn_term = jnp.dot(head_rows, w_out, preferred_element_type=jnp.float32).astype(jnp.bfloat16)
    attn_blocks = attn_term.reshape(chip_count, core_count, row_count, model_width)
    keep = lax.dynamic_index_in_dim(attn_blocks, core_index, axis=1, keepdims=False)
    give = lax.dynamic_index_in_dim(attn_blocks, 1 - core_index, axis=1, keepdims=False)
    given = lax.ppermute(give, "hc", [(0, 1), (1, 0)])
    attn_chip = (keep.astype(jnp.float32) + given.astype(jnp.float32)).astype(jnp.bfloat16)
    attn_parts = lax.all_to_all(attn_chip, "hx", split_axis=0, concat_axis=0, tiled=True)
    attn_own = jnp.sum(attn_parts.astype(jnp.float32), axis=0)
    own_start = head_index * row_count
    hidden_own = lax.dynamic_slice_in_dim(hidden_in, own_start, row_count, 0)
    residual_own = (hidden_own.astype(jnp.float32) + attn_own).astype(jnp.bfloat16)
    normed_own = rms_scale(residual_own.astype(jnp.float32), post_gain).astype(jnp.bfloat16)
    normed_all = lax.all_gather(normed_own, ("hx", "hc"), axis=0, tiled=True)
    swap = [(0, 1), (1, 0)]
    gate_other = lax.ppermute(expert_gate[0], "hc", swap)
    up_other = lax.ppermute(expert_up[0], "hc", swap)
    down_other = lax.ppermute(expert_down[0], "hc", swap)

    gate_other, up_other, down_other, normed_own = lax.optimization_barrier(
        (gate_other, up_other, down_other, normed_own)
    )
    experts = EXPERTS
    capacity = CAP
    logits = jnp.dot(normed_own, w_router, preferred_element_type=jnp.float32)
    matches = routes[:, :, None] == jnp.arange(experts, dtype=jnp.int32)[None, None, :]
    chosen = jnp.sum(jnp.where(matches, logits[:, None, :], 0.0), axis=-1)
    route_weight = jax.nn.softmax(chosen, axis=-1)
    pair_hits = matches.reshape(row_count * top_count, experts).astype(jnp.int32)
    pair_ranks = jnp.cumsum(pair_hits, axis=0) - pair_hits
    slot_of = jnp.sum(pair_ranks * pair_hits, axis=-1)
    slot_width = -(-capacity // 16) * 16
    target = (routes.reshape(-1) * slot_width + slot_of).reshape(row_count, top_count)
    chips = ("req", "hx")
    chip_total = lax.axis_size(chips)
    dest_ids = jnp.arange(chip_total, dtype=jnp.int32)[:, None] * slot_width + jnp.arange(
        slot_width, dtype=jnp.int32
    )[None, :]
    hit = target[:, :, None, None] == dest_ids[None, None, :, :]
    dispatch = jnp.any(hit, axis=1).astype(jnp.bfloat16)
    outgoing = jnp.einsum(
        "tpj,td->pjd", dispatch, normed_own, preferred_element_type=jnp.float32
    ).astype(jnp.bfloat16)
    arrived = lax.all_to_all(outgoing, chips, split_axis=0, concat_axis=0, tiled=True)
    normed_all, arrived = lax.optimization_barrier((normed_all, arrived))
    normed = (
        normed_all.reshape(chip_count, core_count, row_count, model_width)
        .transpose(1, 0, 2, 3)
        .reshape(request_rows, model_width)
    )
    shared_act = (
        jax.nn.silu(jnp.dot(normed, shared_gate, preferred_element_type=jnp.float32))
        * jnp.dot(normed, shared_up, preferred_element_type=jnp.float32)
    ).astype(jnp.bfloat16)
    shared_part = jnp.dot(shared_act, shared_down, preferred_element_type=jnp.float32)
    shared_core = lax.psum_scatter(
        shared_part.astype(jnp.bfloat16), "hc", scatter_dimension=0, tiled=True
    )
    shared_own = lax.psum_scatter(shared_core, "hx", scatter_dimension=0, tiled=True).astype(
        jnp.float32
    )
    def expert_act(rows, gate_w, up_w):
        gate_values = jnp.einsum("pjd,df->pjf", rows, gate_w, preferred_element_type=jnp.float32)
        upward = jnp.einsum("pjd,df->pjf", rows, up_w, preferred_element_type=jnp.float32)
        return (jax.nn.silu(gate_values) * upward).astype(jnp.bfloat16)

    act_own = expert_act(arrived, expert_gate[0], expert_up[0])
    act_other = expert_act(arrived, gate_other, up_other)
    expert_done = (
        jnp.einsum("pjf,fd->pjd", act_own, expert_down[0], preferred_element_type=jnp.float32)
        + jnp.einsum("pjf,fd->pjd", act_other, down_other, preferred_element_type=jnp.float32)
    ).astype(jnp.bfloat16)
    returned = lax.all_to_all(expert_done, chips, split_axis=0, concat_axis=0, tiled=True)
    combine = jnp.sum(jnp.where(hit, route_weight[:, :, None, None], 0.0), axis=1)
    routed = jnp.einsum(
        "tpj,pjd->td",
        combine,
        returned.astype(jnp.float32),
        precision=lax.Precision.HIGHEST,
        preferred_element_type=jnp.float32,
    )
    return (residual_own.astype(jnp.float32) + shared_own + routed).astype(jnp.bfloat16)


def solution(mesh):
    core_count = 2
    split_mesh = jax.sharding.Mesh(
        mesh.devices.reshape(
            mesh.shape["req"], mesh.shape["head"] // core_count, core_count
        ),
        ("req", "hx", "hc"),
    )
    head = ("hx", "hc")
    every = ("req", "hx", "hc")
    in_specs = (
        P("req", None),
        P("req", None, None),
        P("req", None, None),
        P("req"),
        P(),
        P(None, head),
        P(),
        P(),
        P(),
        P(None, head),
        P(None, head),
        P(head, None),
        P(),
        P(),
        P(every, None),
        P(None, head),
        P(None, head),
        P(head, None),
        P(every, None, None),
        P(every, None, None),
        P(every, None, None),
    )
    out_specs = P(every, None)
    return jax.shard_map(
        per_device, mesh=split_mesh, in_specs=in_specs, out_specs=out_specs, check_vma=False
    )
```

```python
import math

import jax
import jax.numpy as jnp
from jax import lax
from jax.sharding import PartitionSpec as P

NOPE = 128
ROPE = 64
VDIM = 128
LATENT = 512
EXPERTS = 64
CAP = 14


def rms_scale(values, gain_row):
    return values * lax.rsqrt(jnp.mean(values * values, axis=-1, keepdims=True) + 1e-06) * gain_row


def rotate(values, positions):
    half_size = values.shape[-1] // 2
    frequency = jnp.exp(
        jnp.arange(half_size, dtype=jnp.float32) * (-2.0 * math.log(10000.0) / values.shape[-1])
    )
    angles = positions.astype(jnp.float32)[:, None] * frequency[None, :]
    shape_mid = (angles.shape[0],) + (1,) * (values.ndim - 2) + (half_size,)
    cosine = jnp.cos(angles).reshape(shape_mid)
    sine_part = jnp.sin(angles).reshape(shape_mid)
    first_half = values[..., :half_size]
    second_half = values[..., half_size:]
    return jnp.concatenate(
        [
            first_half * cosine - second_half * sine_part,
            second_half * cosine + first_half * sine_part,
        ],
        axis=-1,
    )


def attend_rows(absorbed, query_rope, first_row, cache_lat, cache_keys, length, new_latent, new_rope):
    query_count = absorbed.shape[0]
    cache_rows = cache_lat.shape[0]
    score_scale = (NOPE + ROPE) ** (-0.5)
    seen_new = first_row + query_count
    keys_latent = jnp.concatenate([cache_lat, new_latent[:seen_new]], axis=0)
    keys_rope = jnp.concatenate([cache_keys, new_rope[:seen_new]], axis=0)
    scores = (
        jnp.einsum("qhl,kl->qhk", absorbed, keys_latent, preferred_element_type=jnp.float32)
        + jnp.einsum("qhr,kr->qhk", query_rope, keys_rope, preferred_element_type=jnp.float32)
    ) * score_scale
    key_index = jnp.arange(cache_rows + seen_new, dtype=jnp.int32)[None, :]
    query_pos = first_row + jnp.arange(query_count, dtype=jnp.int32)[:, None]
    visible = jnp.where(
        key_index < cache_rows, key_index < length, key_index - cache_rows <= query_pos
    )
    scores = jnp.where(visible[:, None, :], scores, -jnp.inf)
    row_max = jnp.max(scores, axis=-1)
    exponent = jnp.exp(scores - row_max[..., None])
    row_total = jnp.sum(exponent, axis=-1)
    weighted = jnp.einsum(
        "qhk,kl->qhl",
        exponent.astype(jnp.bfloat16),
        keys_latent,
        preferred_element_type=jnp.float32,
    )
    return (weighted / row_total[..., None]).astype(jnp.bfloat16)


def per_device(
    hidden_in,
    cache_latent,
    cache_rope,
    cache_lengths,
    attn_gain,
    w_query,
    w_latent,
    w_latent_rope,
    latent_gain,
    w_key_up,
    w_value_up,
    w_out,
    post_gain,
    w_router,
    routes,
    shared_gate,
    shared_up,
    shared_down,
    expert_gate,
    expert_up,
    expert_down,
):
    request_rows = hidden_in.shape[0]
    model_width = hidden_in.shape[1]
    row_count = routes.shape[0]
    top_count = routes.shape[1]
    head_local = w_query.shape[1] // (NOPE + ROPE)
    length = cache_lengths[0]
    chip_count = lax.axis_size("hx")
    core_count = lax.axis_size("hc")
    chip_index = lax.axis_index("hx")
    core_index = lax.axis_index("hc")
    normed_in = rms_scale(hidden_in.astype(jnp.float32), attn_gain).astype(jnp.bfloat16)
    positions = length + jnp.arange(request_rows, dtype=jnp.int32)
    query_all = jnp.dot(normed_in, w_query, preferred_element_type=jnp.float32).reshape(
        request_rows, head_local, NOPE + ROPE
    )
    query_nope = query_all[..., :NOPE].astype(jnp.bfloat16)
    query_rope = rotate(query_all[..., NOPE:], positions).astype(jnp.bfloat16)
    new_latent = rms_scale(
        jnp.dot(normed_in, w_latent, preferred_element_type=jnp.float32), latent_gain
    ).astype(jnp.bfloat16)
    new_rope = rotate(
        jnp.dot(normed_in, w_latent_rope, preferred_element_type=jnp.float32), positions
    ).astype(jnp.bfloat16)
    key_up = w_key_up.reshape(LATENT, head_local, NOPE)
    absorbed = jnp.einsum(
        "chn,lhn->chl", query_nope, key_up, preferred_element_type=jnp.float32
    ).astype(jnp.bfloat16)
    value_up = w_value_up.reshape(LATENT, head_local, VDIM)
    block_rows = min(512, request_rows)
    outputs = []
    for first_row in range(0, request_rows, block_rows):
        latent_out = attend_rows(
            absorbed[first_row : first_row + block_rows],
            query_rope[first_row : first_row + block_rows],
            first_row,
            cache_latent[0],
            cache_rope[0],
            length,
            new_latent,
            new_rope,
        )
        head_out = jnp.einsum(
            "qhl,lhv->qhv", latent_out, value_up, preferred_element_type=jnp.float32
        ).astype(jnp.bfloat16)
        outputs.append(head_out.reshape(block_rows, head_local * VDIM))
    head_rows = jnp.concatenate(outputs, axis=0)
    head_count = chip_count * core_count
    head_index = chip_index * core_count + core_index
    attn_term = jnp.dot(head_rows, w_out, preferred_element_type=jnp.float32).astype(jnp.bfloat16)
    attn_blocks = attn_term.reshape(chip_count, core_count, row_count, model_width)
    keep = lax.dynamic_index_in_dim(attn_blocks, core_index, axis=1, keepdims=False)
    give = lax.dynamic_index_in_dim(attn_blocks, 1 - core_index, axis=1, keepdims=False)
    given = lax.ppermute(give, "hc", [(0, 1), (1, 0)])
    attn_chip = (keep.astype(jnp.float32) + given.astype(jnp.float32)).astype(jnp.bfloat16)
    attn_parts = lax.all_to_all(attn_chip, "hx", split_axis=0, concat_axis=0, tiled=True)
    attn_own = jnp.sum(attn_parts.astype(jnp.float32), axis=0)
    own_start = head_index * row_count
    hidden_own = lax.dynamic_slice_in_dim(hidden_in, own_start, row_count, 0)
    residual_own = (hidden_own.astype(jnp.float32) + attn_own).astype(jnp.bfloat16)
    normed_own = rms_scale(residual_own.astype(jnp.float32), post_gain).astype(jnp.bfloat16)
    normed_all = lax.all_gather(normed_own, ("hc", "hx"), axis=0, tiled=True)
    swap = [(0, 1), (1, 0)]
    gate_other = lax.ppermute(expert_gate[0], "hc", swap)
    up_other = lax.ppermute(expert_up[0], "hc", swap)
    down_other = lax.ppermute(expert_down[0], "hc", swap)

    gate_other, up_other, down_other, normed_own = lax.optimization_barrier(
        (gate_other, up_other, down_other, normed_own)
    )
    experts = EXPERTS
    capacity = CAP
    logits = jnp.dot(normed_own, w_router, preferred_element_type=jnp.float32)
    matches = routes[:, :, None] == jnp.arange(experts, dtype=jnp.int32)[None, None, :]
    chosen = jnp.sum(jnp.where(matches, logits[:, None, :], 0.0), axis=-1)
    route_weight = jax.nn.softmax(chosen, axis=-1)
    pair_hits = matches.reshape(row_count * top_count, experts).astype(jnp.int32)
    pair_ranks = jnp.cumsum(pair_hits, axis=0) - pair_hits
    slot_of = jnp.sum(pair_ranks * pair_hits, axis=-1)
    slot_width = -(-capacity // 16) * 16
    target = (routes.reshape(-1) * slot_width + slot_of).reshape(row_count, top_count)
    chips = ("req", "hx")
    chip_total = lax.axis_size(chips)
    dest_ids = jnp.arange(chip_total, dtype=jnp.int32)[:, None] * slot_width + jnp.arange(
        slot_width, dtype=jnp.int32
    )[None, :]
    hit = target[:, :, None, None] == dest_ids[None, None, :, :]
    dispatch = jnp.any(hit, axis=1).astype(jnp.bfloat16)
    outgoing = jnp.einsum(
        "tpj,td->pjd", dispatch, normed_own, preferred_element_type=jnp.float32
    ).astype(jnp.bfloat16)
    arrived = lax.all_to_all(outgoing, chips, split_axis=0, concat_axis=0, tiled=True)
    normed_all, arrived = lax.optimization_barrier((normed_all, arrived))
    normed = normed_all
    shared_act = (
        jax.nn.silu(jnp.dot(normed, shared_gate, preferred_element_type=jnp.float32))
        * jnp.dot(normed, shared_up, preferred_element_type=jnp.float32)
    ).astype(jnp.bfloat16)
    shared_part = jnp.dot(shared_act, shared_down, preferred_element_type=jnp.float32)
    shared_core = lax.psum_scatter(
        shared_part.astype(jnp.bfloat16), "hc", scatter_dimension=0, tiled=True
    )
    shared_own = lax.psum_scatter(shared_core, "hx", scatter_dimension=0, tiled=True).astype(
        jnp.float32
    )
    def expert_act(rows, gate_w, up_w):
        gate_values = jnp.einsum("pjd,df->pjf", rows, gate_w, preferred_element_type=jnp.float32)
        upward = jnp.einsum("pjd,df->pjf", rows, up_w, preferred_element_type=jnp.float32)
        return (jax.nn.silu(gate_values) * upward).astype(jnp.bfloat16)

    act_own = expert_act(arrived, expert_gate[0], expert_up[0])
    act_other = expert_act(arrived, gate_other, up_other)
    expert_done = (
        jnp.einsum("pjf,fd->pjd", act_own, expert_down[0], preferred_element_type=jnp.float32)
        + jnp.einsum("pjf,fd->pjd", act_other, down_other, preferred_element_type=jnp.float32)
    ).astype(jnp.bfloat16)
    returned = lax.all_to_all(expert_done, chips, split_axis=0, concat_axis=0, tiled=True)
    combine = jnp.sum(jnp.where(hit, route_weight[:, :, None, None], 0.0), axis=1)
    routed = jnp.einsum(
        "tpj,pjd->td",
        combine,
        returned.astype(jnp.float32),
        precision=lax.Precision.HIGHEST,
        preferred_element_type=jnp.float32,
    )
    return (residual_own.astype(jnp.float32) + shared_own + routed).astype(jnp.bfloat16)


def solution(mesh):
    core_count = 2
    split_mesh = jax.sharding.Mesh(
        mesh.devices.reshape(
            mesh.shape["req"], mesh.shape["head"] // core_count, core_count
        ),
        ("req", "hx", "hc"),
    )
    head = ("hx", "hc")
    every = ("req", "hx", "hc")
    in_specs = (
        P("req", None),
        P("req", None, None),
        P("req", None, None),
        P("req"),
        P(),
        P(None, head),
        P(),
        P(),
        P(),
        P(None, head),
        P(None, head),
        P(head, None),
        P(),
        P(),
        P(every, None),
        P(None, head),
        P(None, head),
        P(head, None),
        P(every, None, None),
        P(every, None, None),
        P(every, None, None),
    )
    out_specs = P(every, None)
    return jax.shard_map(
        per_device, mesh=split_mesh, in_specs=in_specs, out_specs=out_specs, check_vma=False
    )
```

```python
import math

import jax
import jax.numpy as jnp
from jax import lax
from jax.sharding import PartitionSpec as P

NOPE = 128
ROPE = 64
VDIM = 128
LATENT = 512
EXPERTS = 64
CAP = 14


def rms_scale(values, gain_row):
    return values * lax.rsqrt(jnp.mean(values * values, axis=-1, keepdims=True) + 1e-06) * gain_row


def rotate(values, positions):
    half_size = values.shape[-1] // 2
    frequency = jnp.exp(
        jnp.arange(half_size, dtype=jnp.float32) * (-2.0 * math.log(10000.0) / values.shape[-1])
    )
    angles = positions.astype(jnp.float32)[:, None] * frequency[None, :]
    shape_mid = (angles.shape[0],) + (1,) * (values.ndim - 2) + (half_size,)
    cosine = jnp.cos(angles).reshape(shape_mid)
    sine_part = jnp.sin(angles).reshape(shape_mid)
    first_half = values[..., :half_size]
    second_half = values[..., half_size:]
    return jnp.concatenate(
        [
            first_half * cosine - second_half * sine_part,
            second_half * cosine + first_half * sine_part,
        ],
        axis=-1,
    )


def attend_rows(absorbed, query_rope, first_row, cache_lat, cache_keys, length, new_latent, new_rope):
    query_count = absorbed.shape[0]
    cache_rows = cache_lat.shape[0]
    score_scale = (NOPE + ROPE) ** (-0.5)
    seen_new = first_row + query_count
    keys_latent = jnp.concatenate([cache_lat, new_latent[:seen_new]], axis=0)
    keys_rope = jnp.concatenate([cache_keys, new_rope[:seen_new]], axis=0)
    scores = (
        jnp.einsum("qhl,kl->qhk", absorbed, keys_latent, preferred_element_type=jnp.float32)
        + jnp.einsum("qhr,kr->qhk", query_rope, keys_rope, preferred_element_type=jnp.float32)
    ) * score_scale
    key_index = jnp.arange(cache_rows + seen_new, dtype=jnp.int32)[None, :]
    query_pos = first_row + jnp.arange(query_count, dtype=jnp.int32)[:, None]
    visible = jnp.where(
        key_index < cache_rows, key_index < length, key_index - cache_rows <= query_pos
    )
    scores = jnp.where(visible[:, None, :], scores, -jnp.inf)
    row_max = jnp.max(scores, axis=-1)
    exponent = jnp.exp(scores - row_max[..., None])
    row_total = jnp.sum(exponent, axis=-1)
    weighted = jnp.einsum(
        "qhk,kl->qhl",
        exponent.astype(jnp.bfloat16),
        keys_latent,
        preferred_element_type=jnp.float32,
    )
    return (weighted / row_total[..., None]).astype(jnp.bfloat16)


def per_device(
    hidden_in,
    cache_latent,
    cache_rope,
    cache_lengths,
    attn_gain,
    w_query,
    w_latent,
    w_latent_rope,
    latent_gain,
    w_key_up,
    w_value_up,
    w_out,
    post_gain,
    w_router,
    routes,
    shared_gate,
    shared_up,
    shared_down,
    expert_gate,
    expert_up,
    expert_down,
):
    request_rows = hidden_in.shape[0]
    model_width = hidden_in.shape[1]
    row_count = routes.shape[0]
    top_count = routes.shape[1]
    head_local = w_query.shape[1] // (NOPE + ROPE)
    length = cache_lengths[0]
    chip_count = lax.axis_size("hx")
    core_count = lax.axis_size("hc")
    chip_index = lax.axis_index("hx")
    core_index = lax.axis_index("hc")
    normed_in = rms_scale(hidden_in.astype(jnp.float32), attn_gain).astype(jnp.bfloat16)
    positions = length + jnp.arange(request_rows, dtype=jnp.int32)
    query_all = jnp.dot(normed_in, w_query, preferred_element_type=jnp.float32).reshape(
        request_rows, head_local, NOPE + ROPE
    )
    query_nope = query_all[..., :NOPE].astype(jnp.bfloat16)
    query_rope = rotate(query_all[..., NOPE:], positions).astype(jnp.bfloat16)
    new_latent = rms_scale(
        jnp.dot(normed_in, w_latent, preferred_element_type=jnp.float32), latent_gain
    ).astype(jnp.bfloat16)
    new_rope = rotate(
        jnp.dot(normed_in, w_latent_rope, preferred_element_type=jnp.float32), positions
    ).astype(jnp.bfloat16)
    key_up = w_key_up.reshape(LATENT, head_local, NOPE)
    absorbed = jnp.einsum(
        "chn,lhn->chl", query_nope, key_up, preferred_element_type=jnp.float32
    ).astype(jnp.bfloat16)
    value_up = w_value_up.reshape(LATENT, head_local, VDIM)
    block_rows = min(512, request_rows)
    outputs = []
    for first_row in range(0, request_rows, block_rows):
        latent_out = attend_rows(
            absorbed[first_row : first_row + block_rows],
            query_rope[first_row : first_row + block_rows],
            first_row,
            cache_latent[0],
            cache_rope[0],
            length,
            new_latent,
            new_rope,
        )
        head_out = jnp.einsum(
            "qhl,lhv->qhv", latent_out, value_up, preferred_element_type=jnp.float32
        ).astype(jnp.bfloat16)
        outputs.append(head_out.reshape(block_rows, head_local * VDIM))
    head_rows = jnp.concatenate(outputs, axis=0)
    head_count = chip_count * core_count
    head_index = chip_index * core_count + core_index
    attn_term = jnp.dot(head_rows, w_out, preferred_element_type=jnp.float32).astype(jnp.bfloat16)
    attn_blocks = attn_term.reshape(chip_count, core_count, row_count, model_width)
    keep = lax.dynamic_index_in_dim(attn_blocks, core_index, axis=1, keepdims=False)
    give = lax.dynamic_index_in_dim(attn_blocks, 1 - core_index, axis=1, keepdims=False)
    given = lax.ppermute(give, "hc", [(0, 1), (1, 0)])
    attn_chip = (keep.astype(jnp.float32) + given.astype(jnp.float32)).astype(jnp.bfloat16)
    attn_parts = lax.all_to_all(attn_chip, "hx", split_axis=0, concat_axis=0, tiled=True)
    attn_own = jnp.sum(attn_parts.astype(jnp.float32), axis=0)
    own_start = head_index * row_count
    hidden_own = lax.dynamic_slice_in_dim(hidden_in, own_start, row_count, 0)
    residual_own = (hidden_own.astype(jnp.float32) + attn_own).astype(jnp.bfloat16)
    normed_own = rms_scale(residual_own.astype(jnp.float32), post_gain).astype(jnp.bfloat16)
    normed_all = lax.all_gather(normed_own, ("hc", "hx"), axis=0, tiled=True)
    swap = [(0, 1), (1, 0)]
    gate_other = lax.ppermute(expert_gate[0], "hc", swap)
    up_other = lax.ppermute(expert_up[0], "hc", swap)
    down_other = lax.ppermute(expert_down[0], "hc", swap)

    gate_other, up_other, down_other, normed_own = lax.optimization_barrier(
        (gate_other, up_other, down_other, normed_own)
    )
    experts = EXPERTS
    capacity = CAP
    logits = jnp.dot(normed_own, w_router, preferred_element_type=jnp.float32)
    matches = routes[:, :, None] == jnp.arange(experts, dtype=jnp.int32)[None, None, :]
    chosen = jnp.sum(jnp.where(matches, logits[:, None, :], 0.0), axis=-1)
    route_weight = jax.nn.softmax(chosen, axis=-1)
    pair_hits = matches.reshape(row_count * top_count, experts).astype(jnp.int32)
    pair_ranks = jnp.cumsum(pair_hits, axis=0) - pair_hits
    slot_of = jnp.sum(pair_ranks * pair_hits, axis=-1)
    slot_width = -(-capacity // 16) * 16
    target = (routes.reshape(-1) * slot_width + slot_of).reshape(row_count, top_count)
    chips = ("req", "hx")
    chip_total = lax.axis_size(chips)
    dest_ids = jnp.arange(chip_total, dtype=jnp.int32)[:, None] * slot_width + jnp.arange(
        slot_width, dtype=jnp.int32
    )[None, :]
    hit = target[:, :, None, None] == dest_ids[None, None, :, :]
    dispatch = jnp.any(hit, axis=1).astype(jnp.bfloat16)
    outgoing = jnp.einsum(
        "tpj,td->pjd", dispatch, normed_own, preferred_element_type=jnp.float32
    ).astype(jnp.bfloat16)
    arrived = lax.all_to_all(outgoing, chips, split_axis=0, concat_axis=0, tiled=True)
    normed_all, arrived = lax.optimization_barrier((normed_all, arrived))
    normed = normed_all
    shared_act = (
        jax.nn.silu(jnp.dot(normed, shared_gate, preferred_element_type=jnp.float32))
        * jnp.dot(normed, shared_up, preferred_element_type=jnp.float32)
    ).astype(jnp.bfloat16)
    shared_part = jnp.dot(shared_act, shared_down, preferred_element_type=jnp.float32)
    shared_core = lax.psum_scatter(
        shared_part.astype(jnp.bfloat16), "hc", scatter_dimension=0, tiled=True
    )
    shared_own = lax.psum_scatter(shared_core, "hx", scatter_dimension=0, tiled=True).astype(
        jnp.float32
    )
    def expert_act(rows, gate_w, up_w):
        gate_values = jnp.dot(rows, gate_w, preferred_element_type=jnp.float32)
        upward = jnp.dot(rows, up_w, preferred_element_type=jnp.float32)
        return (jax.nn.silu(gate_values) * upward).astype(jnp.bfloat16)

    arrived_rows = arrived.reshape(chip_total * slot_width, model_width)
    act_own = expert_act(arrived_rows, expert_gate[0], expert_up[0])
    act_other = expert_act(arrived_rows, gate_other, up_other)
    expert_done = (
        jnp.dot(act_own, expert_down[0], preferred_element_type=jnp.float32)
        + jnp.dot(act_other, down_other, preferred_element_type=jnp.float32)
    ).astype(jnp.bfloat16).reshape(chip_total, slot_width, model_width)
    returned = lax.all_to_all(expert_done, chips, split_axis=0, concat_axis=0, tiled=True)
    combine = jnp.sum(jnp.where(hit, route_weight[:, :, None, None], 0.0), axis=1)
    routed = jnp.einsum(
        "tpj,pjd->td",
        combine,
        returned.astype(jnp.float32),
        precision=lax.Precision.HIGHEST,
        preferred_element_type=jnp.float32,
    )
    return (residual_own.astype(jnp.float32) + shared_own + routed).astype(jnp.bfloat16)


def solution(mesh):
    core_count = 2
    split_mesh = jax.sharding.Mesh(
        mesh.devices.reshape(
            mesh.shape["req"], mesh.shape["head"] // core_count, core_count
        ),
        ("req", "hx", "hc"),
    )
    head = ("hx", "hc")
    every = ("req", "hx", "hc")
    in_specs = (
        P("req", None),
        P("req", None, None),
        P("req", None, None),
        P("req"),
        P(),
        P(None, head),
        P(),
        P(),
        P(),
        P(None, head),
        P(None, head),
        P(head, None),
        P(),
        P(),
        P(every, None),
        P(None, head),
        P(None, head),
        P(head, None),
        P(every, None, None),
        P(every, None, None),
        P(every, None, None),
    )
    out_specs = P(every, None)
    return jax.shard_map(
        per_device, mesh=split_mesh, in_specs=in_specs, out_specs=out_specs, check_vma=False
    )
```

```python
import math

import jax
import jax.numpy as jnp
from jax import lax
from jax.sharding import PartitionSpec as P

NOPE = 128
ROPE = 64
VDIM = 128
LATENT = 512
EXPERTS = 64
CAP = 14


def rms_scale(values, gain_row):
    return values * lax.rsqrt(jnp.mean(values * values, axis=-1, keepdims=True) + 1e-06) * gain_row


def rotate(values, positions):
    half_size = values.shape[-1] // 2
    frequency = jnp.exp(
        jnp.arange(half_size, dtype=jnp.float32) * (-2.0 * math.log(10000.0) / values.shape[-1])
    )
    angles = positions.astype(jnp.float32)[:, None] * frequency[None, :]
    shape_mid = (angles.shape[0],) + (1,) * (values.ndim - 2) + (half_size,)
    cosine = jnp.cos(angles).reshape(shape_mid)
    sine_part = jnp.sin(angles).reshape(shape_mid)
    first_half = values[..., :half_size]
    second_half = values[..., half_size:]
    return jnp.concatenate(
        [
            first_half * cosine - second_half * sine_part,
            second_half * cosine + first_half * sine_part,
        ],
        axis=-1,
    )


def attend_rows(absorbed, query_rope, first_row, cache_lat, cache_keys, length, new_latent, new_rope):
    query_count = absorbed.shape[0]
    cache_rows = cache_lat.shape[0]
    score_scale = (NOPE + ROPE) ** (-0.5)
    seen_new = first_row + query_count
    keys_latent = jnp.concatenate([cache_lat, new_latent[:seen_new]], axis=0)
    keys_rope = jnp.concatenate([cache_keys, new_rope[:seen_new]], axis=0)
    scores = (
        jnp.einsum("qhl,kl->qhk", absorbed, keys_latent, preferred_element_type=jnp.float32)
        + jnp.einsum("qhr,kr->qhk", query_rope, keys_rope, preferred_element_type=jnp.float32)
    ) * score_scale
    key_index = jnp.arange(cache_rows + seen_new, dtype=jnp.int32)[None, :]
    query_pos = first_row + jnp.arange(query_count, dtype=jnp.int32)[:, None]
    visible = jnp.where(
        key_index < cache_rows, key_index < length, key_index - cache_rows <= query_pos
    )
    scores = jnp.where(visible[:, None, :], scores, -jnp.inf)
    row_max = jnp.max(scores, axis=-1)
    exponent = jnp.exp(scores - row_max[..., None])
    row_total = jnp.sum(exponent, axis=-1)
    weighted = jnp.einsum(
        "qhk,kl->qhl",
        exponent.astype(jnp.bfloat16),
        keys_latent,
        preferred_element_type=jnp.float32,
    )
    return (weighted / row_total[..., None]).astype(jnp.bfloat16)


def per_device(
    hidden_in,
    cache_latent,
    cache_rope,
    cache_lengths,
    attn_gain,
    w_query,
    w_latent,
    w_latent_rope,
    latent_gain,
    w_key_up,
    w_value_up,
    w_out,
    post_gain,
    w_router,
    routes,
    shared_gate,
    shared_up,
    shared_down,
    expert_gate,
    expert_up,
    expert_down,
):
    request_rows = hidden_in.shape[0]
    model_width = hidden_in.shape[1]
    row_count = routes.shape[0]
    top_count = routes.shape[1]
    head_local = w_query.shape[1] // (NOPE + ROPE)
    length = cache_lengths[0]
    chip_count = lax.axis_size("hx")
    core_count = lax.axis_size("hc")
    chip_index = lax.axis_index("hx")
    core_index = lax.axis_index("hc")
    normed_in = rms_scale(hidden_in.astype(jnp.float32), attn_gain).astype(jnp.bfloat16)
    positions = length + jnp.arange(request_rows, dtype=jnp.int32)
    query_all = jnp.dot(normed_in, w_query, preferred_element_type=jnp.float32).reshape(
        request_rows, head_local, NOPE + ROPE
    )
    query_nope = query_all[..., :NOPE].astype(jnp.bfloat16)
    query_rope = rotate(query_all[..., NOPE:], positions).astype(jnp.bfloat16)
    new_latent = rms_scale(
        jnp.dot(normed_in, w_latent, preferred_element_type=jnp.float32), latent_gain
    ).astype(jnp.bfloat16)
    new_rope = rotate(
        jnp.dot(normed_in, w_latent_rope, preferred_element_type=jnp.float32), positions
    ).astype(jnp.bfloat16)
    key_up = w_key_up.reshape(LATENT, head_local, NOPE)
    absorbed = jnp.einsum(
        "chn,lhn->chl", query_nope, key_up, preferred_element_type=jnp.float32
    ).astype(jnp.bfloat16)
    value_up = w_value_up.reshape(LATENT, head_local, VDIM)
    block_rows = min(512, request_rows)
    outputs = []
    for first_row in range(0, request_rows, block_rows):
        latent_out = attend_rows(
            absorbed[first_row : first_row + block_rows],
            query_rope[first_row : first_row + block_rows],
            first_row,
            cache_latent[0],
            cache_rope[0],
            length,
            new_latent,
            new_rope,
        )
        head_out = jnp.einsum(
            "qhl,lhv->qhv", latent_out, value_up, preferred_element_type=jnp.float32
        ).astype(jnp.bfloat16)
        outputs.append(head_out.reshape(block_rows, head_local * VDIM))
    head_rows = jnp.concatenate(outputs, axis=0)
    head_count = chip_count * core_count
    head_index = chip_index * core_count + core_index
    attn_term = jnp.dot(head_rows, w_out, preferred_element_type=jnp.float32).astype(jnp.bfloat16)
    attn_blocks = attn_term.reshape(chip_count, core_count, row_count, model_width)
    keep = lax.dynamic_index_in_dim(attn_blocks, core_index, axis=1, keepdims=False)
    give = lax.dynamic_index_in_dim(attn_blocks, 1 - core_index, axis=1, keepdims=False)
    given = lax.ppermute(give, "hc", [(0, 1), (1, 0)])
    attn_chip = (keep.astype(jnp.float32) + given.astype(jnp.float32)).astype(jnp.bfloat16)
    attn_parts = lax.all_to_all(attn_chip, "hx", split_axis=0, concat_axis=0, tiled=True)
    attn_own = jnp.sum(attn_parts.astype(jnp.float32), axis=0)
    own_start = head_index * row_count
    hidden_own = lax.dynamic_slice_in_dim(hidden_in, own_start, row_count, 0)
    residual_own = (hidden_own.astype(jnp.float32) + attn_own).astype(jnp.bfloat16)
    normed_own = rms_scale(residual_own.astype(jnp.float32), post_gain).astype(jnp.bfloat16)
    normed_all = lax.all_gather(normed_own, ("hc", "hx"), axis=0, tiled=True)
    swap = [(0, 1), (1, 0)]
    gate_other = lax.ppermute(expert_gate[0], "hc", swap)
    up_other = lax.ppermute(expert_up[0], "hc", swap)
    down_other = lax.ppermute(expert_down[0], "hc", swap)

    gate_other, up_other, down_other, normed_own = lax.optimization_barrier(
        (gate_other, up_other, down_other, normed_own)
    )
    experts = EXPERTS
    capacity = CAP
    logits = jnp.dot(normed_own, w_router, preferred_element_type=jnp.float32)
    matches = routes[:, :, None] == jnp.arange(experts, dtype=jnp.int32)[None, None, :]
    chosen = jnp.sum(jnp.where(matches, logits[:, None, :], 0.0), axis=-1)
    route_weight = jax.nn.softmax(chosen, axis=-1)
    pair_hits = matches.reshape(row_count * top_count, experts).astype(jnp.int32)
    pair_ranks = jnp.cumsum(pair_hits, axis=0) - pair_hits
    slot_of = jnp.sum(pair_ranks * pair_hits, axis=-1)
    slot_width = -(-capacity // 16) * 16
    target = (routes.reshape(-1) * slot_width + slot_of).reshape(row_count, top_count)
    chips = ("req", "hx")
    chip_total = lax.axis_size(chips)
    dest_ids = jnp.arange(chip_total, dtype=jnp.int32)[:, None] * slot_width + jnp.arange(
        slot_width, dtype=jnp.int32
    )[None, :]
    hit = target[:, :, None, None] == dest_ids[None, None, :, :]
    dispatch = jnp.any(hit, axis=1).astype(jnp.bfloat16)
    outgoing = jnp.einsum(
        "tpj,td->pjd", dispatch, normed_own, preferred_element_type=jnp.float32
    ).astype(jnp.bfloat16)
    arrived = lax.all_to_all(outgoing, chips, split_axis=0, concat_axis=0, tiled=True)
    normed_all, arrived = lax.optimization_barrier((normed_all, arrived))
    normed = normed_all
    shared_act = (
        jax.nn.silu(jnp.dot(normed, shared_gate, preferred_element_type=jnp.float32))
        * jnp.dot(normed, shared_up, preferred_element_type=jnp.float32)
    ).astype(jnp.bfloat16)
    shared_part = jnp.dot(shared_act, shared_down, preferred_element_type=jnp.float32)
    shared_core = lax.psum_scatter(
        shared_part.astype(jnp.bfloat16), "hc", scatter_dimension=0, tiled=True
    )
    shared_own = lax.psum_scatter(shared_core, "hx", scatter_dimension=0, tiled=True).astype(
        jnp.float32
    )
    def expert_act(rows, gate_w, up_w):
        gate_values = jnp.einsum("pjd,df->pjf", rows, gate_w, preferred_element_type=jnp.float32)
        upward = jnp.einsum("pjd,df->pjf", rows, up_w, preferred_element_type=jnp.float32)
        return (jax.nn.silu(gate_values) * upward).astype(jnp.bfloat16)

    act_own = expert_act(arrived, expert_gate[0], expert_up[0])
    act_other = expert_act(arrived, gate_other, up_other)
    expert_done = (
        jnp.einsum("pjf,fd->pjd", act_own, expert_down[0], preferred_element_type=jnp.float32)
        + jnp.einsum("pjf,fd->pjd", act_other, down_other, preferred_element_type=jnp.float32)
    ).astype(jnp.bfloat16)
    returned = lax.all_to_all(expert_done, chips, split_axis=0, concat_axis=0, tiled=True)
    combine = jnp.sum(jnp.where(hit, route_weight[:, :, None, None], 0.0), axis=1)
    routed = jnp.einsum(
        "tpj,pjd->td",
        combine,
        returned.astype(jnp.float32),
        precision=lax.Precision.HIGH,
        preferred_element_type=jnp.float32,
    )
    return (residual_own.astype(jnp.float32) + shared_own + routed).astype(jnp.bfloat16)


def solution(mesh):
    core_count = 2
    split_mesh = jax.sharding.Mesh(
        mesh.devices.reshape(
            mesh.shape["req"], mesh.shape["head"] // core_count, core_count
        ),
        ("req", "hx", "hc"),
    )
    head = ("hx", "hc")
    every = ("req", "hx", "hc")
    in_specs = (
        P("req", None),
        P("req", None, None),
        P("req", None, None),
        P("req"),
        P(),
        P(None, head),
        P(),
        P(),
        P(),
        P(None, head),
        P(None, head),
        P(head, None),
        P(),
        P(),
        P(every, None),
        P(None, head),
        P(None, head),
        P(head, None),
        P(every, None, None),
        P(every, None, None),
        P(every, None, None),
    )
    out_specs = P(every, None)
    return jax.shard_map(
        per_device, mesh=split_mesh, in_specs=in_specs, out_specs=out_specs, check_vma=False
    )
```
